32 devices in a mesh: seq: 8 (over z, y), head: 2 (over x), cfg: 2 (over core).
Axes of the slice: x: 2, y: 2, z: 4, core: 2. Of those that a mesh axis runs over, the one named last changes fastest.
Arguments:
- queries: bfloat16 [6144, 5120], P(('cfg', 'seq'), 'head'), parts along dimension 0, may hold values from -16 to 16
- fresh_key: bfloat16 [6144, 5120], P(('cfg', 'seq'), 'head'), parts along dimension 0, may hold values from -16 to 16
- fresh_value: bfloat16 [6144, 5120], P(('cfg', 'seq'), 'head'), parts along dimension 0, may hold values from -6 to 6
- stale_key: bfloat16 [6144, 5120], P(('cfg', 'seq'), 'head'), parts along dimension 0, may hold values from -6 to 6
- stale_value: bfloat16 [6144, 5120], P(('cfg', 'seq'), 'head'), parts along dimension 0, may hold values from -6 to 6
- slot_tiles: int32 [48], P('cfg'), parts along dimension 0, may hold values from 0 to 23, as said below
- refresh: int32 [48], P('cfg'), parts along dimension 0, may hold values from 0 to 1, as said below
- stale_reads: int32 [16, 24], P('cfg'), parts along dimension 0, may hold values from 0 to 1, as said below
- out_weight: bfloat16 [5120, 5120], P('head'), may hold values from -6 to 6
Outputs:
- mixed: bfloat16 [6144, 5120], P(('cfg', 'seq', 'head')), parts along dimension 0
The draws below stay inside these ranges and needn't reach their ends.
There are 2 independent parts, one for each index of `cfg`. The reference program is written for one: setup_inputs(seed, part) draws one part's arguments, and reference() takes and returns one part's arrays. A program takes and returns all parts, laid end to end along the dimension named above; an argument that names none is the same for every part. Nothing has to cross between parts.
Inputs may be any that keep to these rules, and one draw needn't show every extreme that they name: `slot_tiles`: A permutation of the 24 tiles. Cache slot i lies on index i // 3 of seq; the slots of every index of seq hold at least one tile that is not refreshed. `refresh`: tile t belongs to index t // 3 of seq. Every index of seq owns between 1 and 2 refreshed tiles; some index owns exactly 1 and some exactly 2. `stale_reads`: only tiles that are not refreshed are read. A reader reads at most one tile among the slots of any one index of seq; some reader reads one tile from the slots of every index.
All inputs are finite; a program needn't handle non-finite values.
Results may differ from the reference program's by a relative error of at most 0.019.
Values may be sent and summed in bfloat16 or wider, within the bound.
No kernel may reach another device: no remote copies, remote signals or barrier semaphores. Data moves between devices by JAX's collectives and lax.ppermute only.
A program may use at most 256 MiB of HBM per device.

```python
import jax
import jax.numpy as jnp
from jax import lax

D = 5120
HEADS = 40
HD = 128
TILE = 128
TILE_DEV = 3
TOK_DEV = 384
TOKENS = 3072
TILES = 24
N_SEQ = 8
N_HEAD = 2


def layout(key):
    parts = jax.random.split(jax.random.fold_in(key, 101), 11)
    count = N_SEQ
    place = jnp.arange(TILE_DEV, dtype=jnp.int32)[None, :]
    device = jnp.arange(count, dtype=jnp.int32)[:, None]
    pick = jax.random.randint(parts[0], (count,), 0, TILE_DEV)
    other = jax.random.randint(parts[1], (count,), 0, TILE_DEV - 1)
    forced = (pick + 1 + other) % TILE_DEV
    coins = jax.random.randint(parts[2], (count, TILE_DEV), 0, 2)
    many = jax.random.randint(parts[3], (), 0, count)
    few = (many + 1 + jax.random.randint(parts[4], (), 0, count - 1)) % count
    filled = jnp.where(device == many, 1, jnp.where(device == few, 0, coins))
    fresh = jnp.where(place == forced[:, None], 1, jnp.where(place == pick[:, None], 0, filled))
    refresh = fresh.reshape(TILES).astype(jnp.int32)
    marked = jnp.arange(count, dtype=jnp.int32) * TILE_DEV + pick
    is_marked = jnp.zeros((TILES,), jnp.int32).at[marked].set(1)
    shuffled = jax.random.permutation(parts[5], TILES).astype(jnp.int32)
    ranking = (1 - is_marked) * TILES + shuffled
    order = jnp.argsort(ranking, stable=True).astype(jnp.int32)
    lists = jnp.concatenate([order[:count][:, None], order[count:].reshape(count, TILE_DEV - 1)], axis=1)
    turned = jax.random.randint(parts[6], (count,), 0, TILE_DEV)
    index = (place - turned[:, None]) % TILE_DEV
    slots = jnp.take_along_axis(lists, index, axis=1)
    holder = jnp.arange(count, dtype=jnp.int32)
    first = jax.random.randint(parts[7], (count, count), 0, TILE_DEV)
    candidate = slots[holder[None, :], first]
    fallback = slots[holder, turned][None, :]
    chosen = jnp.where(refresh[candidate] == 0, candidate, fallback)
    rates = jax.random.randint(parts[8], (count,), 3, 11)
    full = jax.random.randint(parts[9], (), 0, count)
    rates = jnp.where(holder == full, 10, rates)
    taken = (jax.random.randint(parts[10], (count, count), 0, 10) < rates[:, None]).astype(jnp.int32)
    rows = jnp.broadcast_to(holder[:, None], (count, count))
    reads = jnp.zeros((count, TILES), jnp.int32).at[rows, chosen].set(taken)
    return (refresh, slots.reshape(TILES).astype(jnp.int32), reads)


def draw_queries(key, part):
    base = jnp.clip(jax.random.normal(jax.random.fold_in(key, 11), (TOKENS, HEADS * HD), jnp.float32), -4.0, 4.0)
    return base.astype(jnp.bfloat16)


def draw_fresh_key(key, part):
    base = jnp.clip(jax.random.normal(jax.random.fold_in(key, 12), (TOKENS, HEADS * HD), jnp.float32), -4.0, 4.0)
    return base.astype(jnp.bfloat16)


def draw_slot_tiles(key, part):
    return layout(key)[1]


def draw_refresh(key, part):
    return layout(key)[0]


def draw_stale_reads(key, part):
    return layout(key)[2]


def block_scale(stream_key, shape, pieces, least, largest):
    def one(position, blocks):
        draws = jax.random.uniform(jax.random.fold_in(jax.random.fold_in(stream_key, 6), position), (blocks,), jnp.float32, least / len(pieces), largest / len(pieces))
        return jnp.repeat(jnp.exp(draws), shape[position] // blocks).reshape((-1,) + (1,) * (len(shape) - position - 1))

    level = one(*pieces[0])
    for cut in pieces[1:]:
        level = level * one(*cut)
    return level


def normal_values(own_key, dims, deviation, limit, cuts=(), kind=jnp.bfloat16):
    values = deviation * jax.random.normal(own_key, dims, jnp.float32)
    if cuts:
        values = values * block_scale(own_key, dims, cuts, -0.22, 0.18)
    return jnp.clip(values, -limit, limit).astype(kind)


def setup_inputs(seed: int = 0, part: int = 0) -> dict:
    key_of = jax.random.split(jax.random.key(seed), 10)
    part_keys = jax.random.split(jax.random.fold_in(key_of[9], part), 10)
    return {
        "queries": draw_queries(jax.random.fold_in(jax.random.fold_in(key_of[9], part), 71), part),
        "fresh_key": draw_fresh_key(jax.random.fold_in(jax.random.fold_in(key_of[9], part), 71), part),
        "fresh_value": normal_values(part_keys[2], (TOKENS, HEADS * HD), 1.0, 6.0, ((0, 8), (1, 2))),
        "stale_key": normal_values(part_keys[3], (TILES * TILE, HEADS * HD), 1.0, 6.0, ((0, 8), (1, 2))),
        "stale_value": normal_values(part_keys[4], (TILES * TILE, HEADS * HD), 1.0, 6.0, ((0, 8), (1, 2))),
        "slot_tiles": draw_slot_tiles(jax.random.fold_in(jax.random.fold_in(key_of[9], part), 71), part),
        "refresh": draw_refresh(jax.random.fold_in(jax.random.fold_in(key_of[9], part), 71), part),
        "stale_reads": draw_stale_reads(jax.random.fold_in(jax.random.fold_in(key_of[9], part), 71), part),
        "out_weight": normal_values(key_of[8], (HEADS * HD, D), ((TOKENS / (2 * HEADS * HD)) ** 0.5), 6.0, ((0, 2),)),
    }


def reference(queries, fresh_key, fresh_value, stale_key, stale_value, slot_tiles, refresh, stale_reads, out_weight):
    width = HEADS * HD
    scale = HD ** -0.5
    fresh_mask = jnp.repeat(refresh, TILE).astype(jnp.float32)
    slot_hit = (slot_tiles[:, None] == jnp.arange(TILES, dtype=jnp.int32)[None, :]).astype(jnp.int32)
    cache_k = stale_key.astype(jnp.float32).reshape(N_SEQ, TILE_DEV, TILE, width)
    cache_v = stale_value.astype(jnp.float32).reshape(N_SEQ, TILE_DEV, TILE, width)
    keys_f = fresh_key.astype(jnp.float32).reshape(TOKENS, HEADS, HD)
    vals_f = fresh_value.astype(jnp.float32).reshape(TOKENS, HEADS, HD)

    def one_reader(reader):
        row = lax.dynamic_slice_in_dim(stale_reads, reader, 1, 0)[0]
        picked = jnp.sum(slot_hit * row[None, :], axis=1).reshape(N_SEQ, TILE_DEV).astype(jnp.float32)
        keys_s = jnp.einsum("hj,hjrc->hrc", picked, cache_k, precision=lax.Precision.HIGHEST).reshape(N_SEQ * TILE, HEADS, HD)
        vals_s = jnp.einsum("hj,hjrc->hrc", picked, cache_v, precision=lax.Precision.HIGHEST).reshape(N_SEQ * TILE, HEADS, HD)
        stale_mask = jnp.repeat(jnp.sum(picked, axis=1), TILE)
        keys_all = jnp.concatenate([keys_f, keys_s], axis=0)
        vals_all = jnp.concatenate([vals_f, vals_s], axis=0)
        mask = jnp.concatenate([fresh_mask, stale_mask], axis=0)
        query = lax.dynamic_slice_in_dim(queries, reader * TOK_DEV, TOK_DEV, 0).astype(jnp.float32).reshape(TOK_DEV, HEADS, HD)
        score = jnp.einsum("qhd,khd->qhk", query, keys_all, precision=lax.Precision.HIGHEST) * scale
        score = jnp.where(mask[None, None, :] > 0, score, -1e30)
        top = jnp.max(score, axis=2, keepdims=True)
        weight = jnp.exp(score - top) * mask[None, None, :]
        total = jnp.sum(weight, axis=2)
        rounded = lax.optimization_barrier(weight.astype(jnp.bfloat16)).astype(jnp.float32)
        summed = jnp.einsum("qhk,khd->qhd", rounded, vals_all, precision=lax.Precision.HIGHEST)
        return (summed / total[:, :, None]).reshape(TOK_DEV, width).astype(jnp.bfloat16)

    attended = lax.map(one_reader, jnp.arange(N_SEQ, dtype=jnp.int32)).reshape(TOKENS, width)
    group = width // N_HEAD
    mixed = jnp.zeros((TOKENS, D), jnp.float32)
    for index in range(N_HEAD):
        partial_sum = jnp.dot(attended[:, index * group:(index + 1) * group], out_weight[index * group:(index + 1) * group], preferred_element_type=jnp.float32)
        mixed = mixed + lax.optimization_barrier(partial_sum.astype(jnp.bfloat16)).astype(jnp.float32)
    return mixed.astype(jnp.bfloat16)
```

```python
import jax
import jax.numpy as jnp
from jax import lax
from jax.experimental import pallas as pl
from jax.experimental.pallas import tpu as pltpu
from jax.sharding import PartitionSpec as P

HD = 128
TILE = 128


NEG = -1e30


def _scores(q_ref, kf0_ref, kf1_ref, ks_ref, j, second, valid):
    sl = slice(j * HD, (j + 1) * HD)
    qj = q_ref[0, :, sl]
    dims = (((1,), (1,)), ((), ()))
    scale = HD ** -0.5
    s0 = lax.dot_general(qj, kf0_ref[0, :, sl], dims, preferred_element_type=jnp.float32) * scale
    s1 = lax.dot_general(qj, kf1_ref[0, :, sl], dims, preferred_element_type=jnp.float32) * scale
    s2 = lax.dot_general(qj, ks_ref[0, :, sl], dims, preferred_element_type=jnp.float32) * scale
    s1 = jnp.where(second > 0, s1, NEG)
    s2 = jnp.where(valid > 0, s2, NEG)
    return s0, s1, s2


def max_kernel(fsel_ref, sidx_ref, sval_ref, q_ref, kf0_ref, kf1_ref, ks_ref, m_ref):
    r = pl.program_id(0)
    heads_here = q_ref.shape[2] // HD
    second = fsel_ref[2]
    valid = sval_ref[r]
    for j in range(heads_here):
        s0, s1, s2 = _scores(q_ref, kf0_ref, kf1_ref, ks_ref, j, second, valid)
        m = jnp.maximum(
            jnp.maximum(jnp.max(s0, axis=1, keepdims=True), jnp.max(s1, axis=1, keepdims=True)),
            jnp.max(s2, axis=1, keepdims=True),
        )
        m_ref[0, :, j : j + 1] = m


def acc_kernel(
    fsel_ref, sidx_ref, sval_ref, q_ref, kf0_ref, kf1_ref, ks_ref, vf0_ref, vf1_ref, vs_ref, m_ref,
    acc_ref, l_ref,
):
    r = pl.program_id(0)
    heads_here = q_ref.shape[2] // HD
    second = fsel_ref[2]
    valid = sval_ref[r]
    for j in range(heads_here):
        sl = slice(j * HD, (j + 1) * HD)
        s0, s1, s2 = _scores(q_ref, kf0_ref, kf1_ref, ks_ref, j, second, valid)
        top = m_ref[0, :, j : j + 1]
        w0 = jnp.exp(s0 - top)
        w1 = jnp.exp(s1 - top)
        w2 = jnp.exp(s2 - top)
        total = (
            jnp.sum(w0, axis=1, keepdims=True)
            + jnp.sum(w1, axis=1, keepdims=True)
            + jnp.sum(w2, axis=1, keepdims=True)
        )
        summed = (
            jnp.dot(w0.astype(jnp.bfloat16), vf0_ref[0, :, sl], preferred_element_type=jnp.float32)
            + jnp.dot(w1.astype(jnp.bfloat16), vf1_ref[0, :, sl], preferred_element_type=jnp.float32)
            + jnp.dot(w2.astype(jnp.bfloat16), vs_ref[0, :, sl], preferred_element_type=jnp.float32)
        )
        acc_ref[0, :, sl] = summed.astype(acc_ref.dtype)
        l_ref[0, :, j : j + 1] = total


def on_device(
    queries,
    fresh_key,
    fresh_value,
    stale_key,
    stale_value,
    slot_tiles,
    refresh,
    stale_reads,
    out_weight,
):
    tokens_here = queries.shape[0]
    width_here = queries.shape[1]
    heads_here = width_here // HD
    tile_dev = tokens_here // TILE
    readers = stale_reads.shape[0]
    me = lax.axis_index("seq")

    my_refresh = lax.dynamic_slice_in_dim(refresh, me * tile_dev, tile_dev, 0)
    first = jnp.argmax(my_refresh).astype(jnp.int32)
    last = (tile_dev - 1 - jnp.argmax(my_refresh[::-1])).astype(jnp.int32)
    second = (jnp.sum(my_refresh) >= 2).astype(jnp.int32)
    fsel = jnp.stack([first, last, second])

    my_slots = lax.dynamic_slice_in_dim(slot_tiles, me * tile_dev, tile_dev, 0)
    wanted = jnp.take(stale_reads, my_slots, axis=1)
    sidx = jnp.argmax(wanted, axis=1).astype(jnp.int32)
    sval = jnp.max(wanted, axis=1).astype(jnp.int32)

    q_all = lax.all_gather(queries, "seq", axis=0, tiled=False)
    fk3 = fresh_key.reshape(tile_dev, TILE, width_here)
    fv3 = fresh_value.reshape(tile_dev, TILE, width_here)
    sk3 = stale_key.reshape(tile_dev, TILE, width_here)
    sv3 = stale_value.reshape(tile_dev, TILE, width_here)

    q_spec = pl.BlockSpec((1, tokens_here, width_here), lambda r, f, s, v: (r, 0, 0))
    f0_spec = pl.BlockSpec((1, TILE, width_here), lambda r, f, s, v: (f[0], 0, 0))
    f1_spec = pl.BlockSpec((1, TILE, width_here), lambda r, f, s, v: (f[1], 0, 0))
    s_spec = pl.BlockSpec((1, TILE, width_here), lambda r, f, s, v: (s[r], 0, 0))
    stat_spec = pl.BlockSpec((1, tokens_here, heads_here), lambda r, f, s, v: (r, 0, 0))
    stat_shape = jax.ShapeDtypeStruct((readers, tokens_here, heads_here), jnp.float32)
    params = pltpu.CompilerParams(dimension_semantics=("arbitrary",))

    local_top = pl.pallas_call(
        max_kernel,
        grid_spec=pltpu.PrefetchScalarGridSpec(
            num_scalar_prefetch=3,
            grid=(readers,),
            in_specs=[q_spec, f0_spec, f1_spec, s_spec],
            out_specs=stat_spec,
        ),
        out_shape=stat_shape,
        compiler_params=params,
    )(fsel, sidx, sval, q_all, fk3, fk3, sk3)
    top = lax.pmax(local_top, "seq")

    summed, total = pl.pallas_call(
        acc_kernel,
        grid_spec=pltpu.PrefetchScalarGridSpec(
            num_scalar_prefetch=3,
            grid=(readers,),
            in_specs=[q_spec, f0_spec, f1_spec, s_spec, f0_spec, f1_spec, s_spec, stat_spec],
            out_specs=[q_spec, stat_spec],
        ),
        out_shape=[
            jax.ShapeDtypeStruct((readers, tokens_here, width_here), jnp.bfloat16),
            stat_shape,
        ],
        compiler_params=params,
    )(fsel, sidx, sval, q_all, fk3, fk3, sk3, fv3, fv3, sv3, top)

    summed = lax.psum_scatter(summed, "seq", scatter_dimension=0, tiled=True)[0]
    total = lax.psum_scatter(total, "seq", scatter_dimension=0, tiled=True)[0]
    attended = (
        (summed.astype(jnp.float32).reshape(tokens_here, heads_here, HD) / total[:, :, None])
        .reshape(tokens_here, width_here)
        .astype(jnp.bfloat16)
    )
    return lax.psum_scatter(
        jnp.dot(attended, out_weight, preferred_element_type=jnp.float32).astype(jnp.bfloat16),
        "head",
        scatter_dimension=0,
        tiled=True,
    )


def solution(mesh):
    return jax.shard_map(
        on_device,
        mesh=mesh,
        in_specs=(
            P(("cfg", "seq"), "head"),
            P(("cfg", "seq"), "head"),
            P(("cfg", "seq"), "head"),
            P(("cfg", "seq"), "head"),
            P(("cfg", "seq"), "head"),
            P("cfg"),
            P("cfg"),
            P("cfg", None),
            P("head", None),
        ),
        out_specs=P(("cfg", "seq", "head"), None),
        check_vma=False,
    )
```

```python
import jax
import jax.numpy as jnp
from jax import lax
from jax.experimental import pallas as pl
from jax.experimental.pallas import tpu as pltpu
from jax.sharding import PartitionSpec as P

HD = 128
TILE = 128


NEG = -1e30


def _scores(q_ref, kf0_ref, kf1_ref, ks_ref, j, second, valid):
    sl = slice(j * HD, (j + 1) * HD)
    qj = q_ref[0, :, sl]
    dims = (((1,), (1,)), ((), ()))
    scale = HD ** -0.5
    s0 = lax.dot_general(kf0_ref[0, :, sl], qj, dims, preferred_element_type=jnp.float32) * scale
    s1 = lax.dot_general(kf1_ref[0, :, sl], qj, dims, preferred_element_type=jnp.float32) * scale
    s2 = lax.dot_general(ks_ref[0, :, sl], qj, dims, preferred_element_type=jnp.float32) * scale
    s1 = jnp.where(second > 0, s1, NEG)
    s2 = jnp.where(valid > 0, s2, NEG)
    return s0, s1, s2


def max_kernel(fsel_ref, sidx_ref, sval_ref, q_ref, kf0_ref, kf1_ref, ks_ref, m_ref):
    r = pl.program_id(0)
    heads_here = q_ref.shape[2] // HD
    second = fsel_ref[2]
    valid = sval_ref[r]
    for j in range(heads_here):
        s0, s1, s2 = _scores(q_ref, kf0_ref, kf1_ref, ks_ref, j, second, valid)
        m = jnp.maximum(
            jnp.maximum(jnp.max(s0, axis=0, keepdims=True), jnp.max(s1, axis=0, keepdims=True)),
            jnp.max(s2, axis=0, keepdims=True),
        )
        m_ref[0, j : j + 1, :] = m


def acc_kernel(
    fsel_ref, sidx_ref, sval_ref, q_ref, kf0_ref, kf1_ref, ks_ref, vf0_ref, vf1_ref, vs_ref, m_ref,
    acc_ref, l_ref,
):
    r = pl.program_id(0)
    heads_here = q_ref.shape[2] // HD
    second = fsel_ref[2]
    valid = sval_ref[r]
    tn = (((0,), (0,)), ((), ()))
    for j in range(heads_here):
        sl = slice(j * HD, (j + 1) * HD)
        s0, s1, s2 = _scores(q_ref, kf0_ref, kf1_ref, ks_ref, j, second, valid)
        top = m_ref[0, j : j + 1, :]
        w0 = jnp.exp(s0 - top)
        w1 = jnp.exp(s1 - top)
        w2 = jnp.exp(s2 - top)
        total = (
            jnp.sum(w0, axis=0, keepdims=True)
            + jnp.sum(w1, axis=0, keepdims=True)
            + jnp.sum(w2, axis=0, keepdims=True)
        )
        summed = (
            lax.dot_general(w0.astype(jnp.bfloat16), vf0_ref[0, :, sl], tn, preferred_element_type=jnp.float32)
            + lax.dot_general(w1.astype(jnp.bfloat16), vf1_ref[0, :, sl], tn, preferred_element_type=jnp.float32)
            + lax.dot_general(w2.astype(jnp.bfloat16), vs_ref[0, :, sl], tn, preferred_element_type=jnp.float32)
        )
        acc_ref[0, :, sl] = summed.astype(acc_ref.dtype)
        l_ref[0, j : j + 1, :] = total


def on_device(
    queries,
    fresh_key,
    fresh_value,
    stale_key,
    stale_value,
    slot_tiles,
    refresh,
    stale_reads,
    out_weight,
):
    tokens_here = queries.shape[0]
    width_here = queries.shape[1]
    heads_here = width_here // HD
    tile_dev = tokens_here // TILE
    readers = stale_reads.shape[0]
    me = lax.axis_index("seq")

    my_refresh = lax.dynamic_slice_in_dim(refresh, me * tile_dev, tile_dev, 0)
    first = jnp.argmax(my_refresh).astype(jnp.int32)
    last = (tile_dev - 1 - jnp.argmax(my_refresh[::-1])).astype(jnp.int32)
    second = (jnp.sum(my_refresh) >= 2).astype(jnp.int32)
    fsel = jnp.stack([first, last, second])

    my_slots = lax.dynamic_slice_in_dim(slot_tiles, me * tile_dev, tile_dev, 0)
    wanted = jnp.take(stale_reads, my_slots, axis=1)
    sidx = jnp.argmax(wanted, axis=1).astype(jnp.int32)
    sval = jnp.max(wanted, axis=1).astype(jnp.int32)

    q_all = lax.all_gather(queries, "seq", axis=0, tiled=False)
    fk3 = fresh_key.reshape(tile_dev, TILE, width_here)
    fv3 = fresh_value.reshape(tile_dev, TILE, width_here)
    sk3 = stale_key.reshape(tile_dev, TILE, width_here)
    sv3 = stale_value.reshape(tile_dev, TILE, width_here)

    q_spec = pl.BlockSpec((1, tokens_here, width_here), lambda r, f, s, v: (r, 0, 0))
    f0_spec = pl.BlockSpec((1, TILE, width_here), lambda r, f, s, v: (f[0], 0, 0))
    f1_spec = pl.BlockSpec((1, TILE, width_here), lambda r, f, s, v: (f[1], 0, 0))
    s_spec = pl.BlockSpec((1, TILE, width_here), lambda r, f, s, v: (s[r], 0, 0))
    stat_spec = pl.BlockSpec((1, heads_here, tokens_here), lambda r, f, s, v: (r, 0, 0))
    stat_shape = jax.ShapeDtypeStruct((readers, heads_here, tokens_here), jnp.float32)
    params = pltpu.CompilerParams(dimension_semantics=("arbitrary",))

    local_top = pl.pallas_call(
        max_kernel,
        grid_spec=pltpu.PrefetchScalarGridSpec(
            num_scalar_prefetch=3,
            grid=(readers,),
            in_specs=[q_spec, f0_spec, f1_spec, s_spec],
            out_specs=stat_spec,
        ),
        out_shape=stat_shape,
        compiler_params=params,
    )(fsel, sidx, sval, q_all, fk3, fk3, sk3)
    top = lax.pmax(local_top, "seq")

    summed, total = pl.pallas_call(
        acc_kernel,
        grid_spec=pltpu.PrefetchScalarGridSpec(
            num_scalar_prefetch=3,
            grid=(readers,),
            in_specs=[q_spec, f0_spec, f1_spec, s_spec, f0_spec, f1_spec, s_spec, stat_spec],
            out_specs=[q_spec, stat_spec],
        ),
        out_shape=[
            jax.ShapeDtypeStruct((readers, tokens_here, width_here), jnp.bfloat16),
            stat_shape,
        ],
        compiler_params=params,
    )(fsel, sidx, sval, q_all, fk3, fk3, sk3, fv3, fv3, sv3, top)

    summed = lax.psum_scatter(summed, "seq", scatter_dimension=0, tiled=True)[0]
    total = lax.psum_scatter(total, "seq", scatter_dimension=0, tiled=True)[0].T
    attended = (
        (summed.astype(jnp.float32).reshape(tokens_here, heads_here, HD) / total[:, :, None])
        .reshape(tokens_here, width_here)
        .astype(jnp.bfloat16)
    )
    return lax.psum_scatter(
        jnp.dot(attended, out_weight, preferred_element_type=jnp.float32).astype(jnp.bfloat16),
        "head",
        scatter_dimension=0,
        tiled=True,
    )


def solution(mesh):
    return jax.shard_map(
        on_device,
        mesh=mesh,
        in_specs=(
            P(("cfg", "seq"), "head"),
            P(("cfg", "seq"), "head"),
            P(("cfg", "seq"), "head"),
            P(("cfg", "seq"), "head"),
            P(("cfg", "seq"), "head"),
            P("cfg"),
            P("cfg"),
            P("cfg", None),
            P("head", None),
        ),
        out_specs=P(("cfg", "seq", "head"), None),
        check_vma=False,
    )
```

```python
import jax
import jax.numpy as jnp
from jax import lax
from jax.experimental import pallas as pl
from jax.experimental.pallas import tpu as pltpu
from jax.sharding import PartitionSpec as P

HD = 128
TILE = 128


NEG = -1e30


def _scores(q_ref, kf0_ref, kf1_ref, ks_ref, j, second, valid):
    sl = slice(j * HD, (j + 1) * HD)
    qj = q_ref[0, :, sl]
    dims = (((1,), (1,)), ((), ()))
    scale = HD ** -0.5
    s0 = lax.dot_general(kf0_ref[0, :, sl], qj, dims, preferred_element_type=jnp.float32) * scale
    s1 = lax.dot_general(kf1_ref[0, :, sl], qj, dims, preferred_element_type=jnp.float32) * scale
    s2 = lax.dot_general(ks_ref[0, :, sl], qj, dims, preferred_element_type=jnp.float32) * scale
    s1 = jnp.where(second > 0, s1, NEG)
    s2 = jnp.where(valid > 0, s2, NEG)
    return s0, s1, s2


def acc_kernel(
    fsel_ref, sidx_ref, sval_ref, q_ref, kf0_ref, kf1_ref, ks_ref, vf0_ref, vf1_ref, vs_ref,
    acc_ref, m_ref, l_ref,
):
    r = pl.program_id(0)
    heads_here = q_ref.shape[2] // HD
    second = fsel_ref[2]
    valid = sval_ref[r]
    tn = (((0,), (0,)), ((), ()))
    for j in range(heads_here):
        sl = slice(j * HD, (j + 1) * HD)
        s0, s1, s2 = _scores(q_ref, kf0_ref, kf1_ref, ks_ref, j, second, valid)
        top = jnp.maximum(
            jnp.maximum(jnp.max(s0, axis=0, keepdims=True), jnp.max(s1, axis=0, keepdims=True)),
            jnp.max(s2, axis=0, keepdims=True),
        )
        w0 = jnp.exp(s0 - top)
        w1 = jnp.exp(s1 - top)
        w2 = jnp.exp(s2 - top)
        total = (
            jnp.sum(w0, axis=0, keepdims=True)
            + jnp.sum(w1, axis=0, keepdims=True)
            + jnp.sum(w2, axis=0, keepdims=True)
        )
        summed = (
            lax.dot_general(w0.astype(jnp.bfloat16), vf0_ref[0, :, sl], tn, preferred_element_type=jnp.float32)
            + lax.dot_general(w1.astype(jnp.bfloat16), vf1_ref[0, :, sl], tn, preferred_element_type=jnp.float32)
            + lax.dot_general(w2.astype(jnp.bfloat16), vs_ref[0, :, sl], tn, preferred_element_type=jnp.float32)
        )
        acc_ref[0, :, sl] = summed.astype(acc_ref.dtype)
        m_ref[0, j : j + 1, :] = top
        l_ref[0, j : j + 1, :] = total


def ring_order(n):
    if n == 8:
        return [0, 2, 4, 6, 7, 5, 3, 1]
    return list(range(n))


def combine(run, mine):
    acc_r, stat_r = run
    acc_o, stat_o = mine
    tokens, width = acc_o.shape
    hh = width // HD
    top = jnp.maximum(stat_r[0], stat_o[0])
    f_r = jnp.exp(stat_r[0] - top)
    f_o = jnp.exp(stat_o[0] - top)
    total = stat_r[1] * f_r + stat_o[1] * f_o
    acc = acc_r.astype(jnp.float32).reshape(tokens, hh, HD) * f_r.T[:, :, None] + acc_o.astype(
        jnp.float32
    ).reshape(tokens, hh, HD) * f_o.T[:, :, None]
    return acc.reshape(tokens, width), jnp.stack([top, total])


def on_device(
    queries,
    fresh_key,
    fresh_value,
    stale_key,
    stale_value,
    slot_tiles,
    refresh,
    stale_reads,
    out_weight,
):
    tokens_here = queries.shape[0]
    width_here = queries.shape[1]
    heads_here = width_here // HD
    tile_dev = tokens_here // TILE
    readers = stale_reads.shape[0]
    me = lax.axis_index("seq")

    my_refresh = lax.dynamic_slice_in_dim(refresh, me * tile_dev, tile_dev, 0)
    first = jnp.argmax(my_refresh).astype(jnp.int32)
    last = (tile_dev - 1 - jnp.argmax(my_refresh[::-1])).astype(jnp.int32)
    second = (jnp.sum(my_refresh) >= 2).astype(jnp.int32)
    fsel = jnp.stack([first, last, second])

    my_slots = lax.dynamic_slice_in_dim(slot_tiles, me * tile_dev, tile_dev, 0)
    wanted = jnp.take(stale_reads, my_slots, axis=1)
    sidx = jnp.argmax(wanted, axis=1).astype(jnp.int32)
    sval = jnp.max(wanted, axis=1).astype(jnp.int32)

    q_all = lax.all_gather(queries, "seq", axis=0, tiled=False)
    fk3 = fresh_key.reshape(tile_dev, TILE, width_here)
    fv3 = fresh_value.reshape(tile_dev, TILE, width_here)
    sk3 = stale_key.reshape(tile_dev, TILE, width_here)
    sv3 = stale_value.reshape(tile_dev, TILE, width_here)

    q_spec = pl.BlockSpec((1, tokens_here, width_here), lambda r, f, s, v: (r, 0, 0))
    f0_spec = pl.BlockSpec((1, TILE, width_here), lambda r, f, s, v: (f[0], 0, 0))
    f1_spec = pl.BlockSpec((1, TILE, width_here), lambda r, f, s, v: (f[1], 0, 0))
    s_spec = pl.BlockSpec((1, TILE, width_here), lambda r, f, s, v: (s[r], 0, 0))
    stat_spec = pl.BlockSpec((1, heads_here, tokens_here), lambda r, f, s, v: (r, 0, 0))
    stat_shape = jax.ShapeDtypeStruct((readers, heads_here, tokens_here), jnp.float32)
    params = pltpu.CompilerParams(dimension_semantics=("arbitrary",))

    summed, top, total = pl.pallas_call(
        acc_kernel,
        grid_spec=pltpu.PrefetchScalarGridSpec(
            num_scalar_prefetch=3,
            grid=(readers,),
            in_specs=[q_spec, f0_spec, f1_spec, s_spec, f0_spec, f1_spec, s_spec],
            out_specs=[q_spec, stat_spec, stat_spec],
        ),
        out_shape=[
            jax.ShapeDtypeStruct((readers, tokens_here, width_here), jnp.bfloat16),
            stat_shape,
            stat_shape,
        ],
        compiler_params=params,
    )(fsel, sidx, sval, q_all, fk3, fk3, sk3, fv3, fv3, sv3)
    stats = jnp.stack([top, total], axis=1)

    ring = ring_order(readers)
    place = [0] * readers
    for i, d in enumerate(ring):
        place[d] = i
    ring_arr = jnp.array(ring, jnp.int32)
    pos = jnp.array(place, jnp.int32)[me]
    forward = [(ring[i], ring[(i + 1) % readers]) for i in range(readers)]
    backward = [(ring[i], ring[(i - 1) % readers]) for i in range(readers)]
    split = heads_here // 2

    def own(at, h0, h1):
        r = ring_arr[at % readers]
        acc = lax.dynamic_index_in_dim(summed, r, 0, keepdims=False)[:, h0 * HD : h1 * HD]
        st = lax.dynamic_index_in_dim(stats, r, 0, keepdims=False)[:, h0:h1]
        return acc, st

    run_f = own(pos - 1 + readers, 0, split)
    run_b = own(pos + 1, split, heads_here)
    for k in range(1, readers):
        got_f = lax.ppermute(run_f, "seq", forward)
        got_b = lax.ppermute(run_b, "seq", backward)
        run_f = combine(got_f, own(pos - 1 - k + 2 * readers, 0, split))
        run_b = combine(got_b, own(pos + 1 + k, split, heads_here))
        if k < readers - 1:
            run_f = (run_f[0].astype(jnp.bfloat16), run_f[1])
            run_b = (run_b[0].astype(jnp.bfloat16), run_b[1])
    acc = jnp.concatenate([run_f[0], run_b[0]], axis=1)
    total = jnp.concatenate([run_f[1][1], run_b[1][1]], axis=0).T
    attended = (
        (acc.reshape(tokens_here, heads_here, HD) / total[:, :, None])
        .reshape(tokens_here, width_here)
        .astype(jnp.bfloat16)
    )
    return lax.psum_scatter(
        jnp.dot(attended, out_weight, preferred_element_type=jnp.float32).astype(jnp.bfloat16),
        "head",
        scatter_dimension=0,
        tiled=True,
    )


def solution(mesh):
    return jax.shard_map(
        on_device,
        mesh=mesh,
        in_specs=(
            P(("cfg", "seq"), "head"),
            P(("cfg", "seq"), "head"),
            P(("cfg", "seq"), "head"),
            P(("cfg", "seq"), "head"),
            P(("cfg", "seq"), "head"),
            P("cfg"),
            P("cfg"),
            P("cfg", None),
            P("head", None),
        ),
        out_specs=P(("cfg", "seq", "head"), None),
        check_vma=False,
    )
```

```python
import jax
import jax.numpy as jnp
from jax import lax
from jax.experimental import pallas as pl
from jax.experimental.pallas import tpu as pltpu
from jax.sharding import PartitionSpec as P

HD = 128
TILE = 128


NEG = -1e30


def _scores(q_ref, kf0_ref, kf1_ref, ks_ref, j, second, valid):
    sl = slice(j * HD, (j + 1) * HD)
    qj = q_ref[0, :, sl]
    dims = (((1,), (1,)), ((), ()))
    scale = HD ** -0.5
    s0 = lax.dot_general(kf0_ref[0, :, sl], qj, dims, preferred_element_type=jnp.float32) * scale
    s1 = lax.dot_general(kf1_ref[0, :, sl], qj, dims, preferred_element_type=jnp.float32) * scale
    s2 = lax.dot_general(ks_ref[0, :, sl], qj, dims, preferred_element_type=jnp.float32) * scale
    s1 = jnp.where(second > 0, s1, NEG)
    s2 = jnp.where(valid > 0, s2, NEG)
    return s0, s1, s2


def acc_kernel(
    fsel_ref, sidx_ref, sval_ref, fslot_ref, bslot_ref,
    q_ref, kf0_ref, kf1_ref, ks_ref, vf0_ref, vf1_ref, vs_ref,
    accf_ref, accb_ref, stf_ref, stb_ref,
):
    r = pl.program_id(0)
    heads_here = q_ref.shape[2] // HD
    split = accf_ref.shape[1] // HD
    second = fsel_ref[2]
    valid = sval_ref[r]
    tn = (((0,), (0,)), ((), ()))
    for j in range(heads_here):
        sl = slice(j * HD, (j + 1) * HD)
        s0, s1, s2 = _scores(q_ref, kf0_ref, kf1_ref, ks_ref, j, second, valid)
        top = jnp.maximum(
            jnp.maximum(jnp.max(s0, axis=0, keepdims=True), jnp.max(s1, axis=0, keepdims=True)),
            jnp.max(s2, axis=0, keepdims=True),
        )
        w0 = jnp.exp(s0 - top)
        w1 = jnp.exp(s1 - top)
        w2 = jnp.exp(s2 - top)
        total = (
            jnp.sum(w0, axis=0, keepdims=True)
            + jnp.sum(w1, axis=0, keepdims=True)
            + jnp.sum(w2, axis=0, keepdims=True)
        )
        summed = (
            lax.dot_general(vf0_ref[0, :, sl], w0.astype(jnp.bfloat16), tn, preferred_element_type=jnp.float32)
            + lax.dot_general(vf1_ref[0, :, sl], w1.astype(jnp.bfloat16), tn, preferred_element_type=jnp.float32)
            + lax.dot_general(vs_ref[0, :, sl], w2.astype(jnp.bfloat16), tn, preferred_element_type=jnp.float32)
        )
        if j < split:
            accf_ref[0, sl, :] = summed.astype(accf_ref.dtype)
            stf_ref[0, 0, j : j + 1, :] = top
            stf_ref[0, 1, j : j + 1, :] = total
        else:
            i = j - split
            accb_ref[0, i * HD : (i + 1) * HD, :] = summed.astype(accb_ref.dtype)
            stb_ref[0, 0, i : i + 1, :] = top
            stb_ref[0, 1, i : i + 1, :] = total


def ring_order(n):
    if n == 8:
        return [0, 2, 4, 6, 7, 5, 3, 1]
    return list(range(n))


def combine(run, mine):
    acc_r, stat_r = run
    acc_o, stat_o = mine
    top = jnp.maximum(stat_r[0], stat_o[0])
    f_r = jnp.exp(stat_r[0] - top)
    f_o = jnp.exp(stat_o[0] - top)
    total = stat_r[1] * f_r + stat_o[1] * f_o
    acc = acc_r.astype(jnp.float32) * jnp.repeat(f_r, HD, axis=0) + acc_o.astype(
        jnp.float32
    ) * jnp.repeat(f_o, HD, axis=0)
    return acc, jnp.stack([top, total])


def on_device(
    queries,
    fresh_key,
    fresh_value,
    stale_key,
    stale_value,
    slot_tiles,
    refresh,
    stale_reads,
    out_weight,
):
    tokens_here = queries.shape[0]
    width_here = queries.shape[1]
    heads_here = width_here // HD
    tile_dev = tokens_here // TILE
    readers = stale_reads.shape[0]
    me = lax.axis_index("seq")

    my_refresh = lax.dynamic_slice_in_dim(refresh, me * tile_dev, tile_dev, 0)
    first = jnp.argmax(my_refresh).astype(jnp.int32)
    last = (tile_dev - 1 - jnp.argmax(my_refresh[::-1])).astype(jnp.int32)
    second = (jnp.sum(my_refresh) >= 2).astype(jnp.int32)
    fsel = jnp.stack([first, last, second])

    my_slots = lax.dynamic_slice_in_dim(slot_tiles, me * tile_dev, tile_dev, 0)
    wanted = jnp.take(stale_reads, my_slots, axis=1)
    sidx = jnp.argmax(wanted, axis=1).astype(jnp.int32)
    sval = jnp.max(wanted, axis=1).astype(jnp.int32)

    q_all = lax.all_gather(queries, "seq", axis=0, tiled=False)
    fk3 = fresh_key.reshape(tile_dev, TILE, width_here)
    fv3 = fresh_value.reshape(tile_dev, TILE, width_here)
    sk3 = stale_key.reshape(tile_dev, TILE, width_here)
    sv3 = stale_value.reshape(tile_dev, TILE, width_here)

    ring = ring_order(readers)
    place = [0] * readers
    for i, d in enumerate(ring):
        place[d] = i
    pos = jnp.array(place, jnp.int32)[me]
    place_arr = jnp.array(place, jnp.int32)
    fslot = (pos - 1 - place_arr + readers) % readers
    bslot = (place_arr - pos - 1 + 2 * readers) % readers
    forward = [(ring[i], ring[(i + 1) % readers]) for i in range(readers)]
    backward = [(ring[i], ring[(i - 1) % readers]) for i in range(readers)]
    split = heads_here // 2
    rest = heads_here - split

    q_spec = pl.BlockSpec((1, tokens_here, width_here), lambda r, f, s, v, a, b: (r, 0, 0))
    f0_spec = pl.BlockSpec((1, TILE, width_here), lambda r, f, s, v, a, b: (f[0], 0, 0))
    f1_spec = pl.BlockSpec((1, TILE, width_here), lambda r, f, s, v, a, b: (f[1], 0, 0))
    s_spec = pl.BlockSpec((1, TILE, width_here), lambda r, f, s, v, a, b: (s[r], 0, 0))
    accf_spec = pl.BlockSpec((1, split * HD, tokens_here), lambda r, f, s, v, a, b: (a[r], 0, 0))
    accb_spec = pl.BlockSpec((1, rest * HD, tokens_here), lambda r, f, s, v, a, b: (b[r], 0, 0))
    stf_spec = pl.BlockSpec((1, 2, split, tokens_here), lambda r, f, s, v, a, b: (a[r], 0, 0, 0))
    stb_spec = pl.BlockSpec((1, 2, rest, tokens_here), lambda r, f, s, v, a, b: (b[r], 0, 0, 0))
    params = pltpu.CompilerParams(dimension_semantics=("arbitrary",))

    acc_f, acc_b, st_f, st_b = pl.pallas_call(
        acc_kernel,
        grid_spec=pltpu.PrefetchScalarGridSpec(
            num_scalar_prefetch=5,
            grid=(readers,),
            in_specs=[q_spec, f0_spec, f1_spec, s_spec, f0_spec, f1_spec, s_spec],
            out_specs=[accf_spec, accb_spec, stf_spec, stb_spec],
        ),
        out_shape=[
            jax.ShapeDtypeStruct((readers, split * HD, tokens_here), jnp.bfloat16),
            jax.ShapeDtypeStruct((readers, rest * HD, tokens_here), jnp.bfloat16),
            jax.ShapeDtypeStruct((readers, 2, split, tokens_here), jnp.float32),
            jax.ShapeDtypeStruct((readers, 2, rest, tokens_here), jnp.float32),
        ],
        compiler_params=params,
    )(fsel, sidx, sval, fslot, bslot, q_all, fk3, fk3, sk3, fv3, fv3, sv3)

    run_f = (acc_f[0], st_f[0])
    run_b = (acc_b[0], st_b[0])
    for k in range(1, readers):
        got_f = lax.ppermute(run_f, "seq", forward)
        got_b = lax.ppermute(run_b, "seq", backward)
        run_f = combine(got_f, (acc_f[k], st_f[k]))
        run_b = combine(got_b, (acc_b[k], st_b[k]))
        if k < readers - 1:
            run_f = (run_f[0].astype(jnp.bfloat16), run_f[1])
            run_b = (run_b[0].astype(jnp.bfloat16), run_b[1])
    acc = jnp.concatenate([run_f[0], run_b[0]], axis=0)
    total = jnp.concatenate([run_f[1][1], run_b[1][1]], axis=0)
    attended = (acc / jnp.repeat(total, HD, axis=0)).astype(jnp.bfloat16)
    mixed = lax.dot_general(
        attended, out_weight, (((0,), (0,)), ((), ())), preferred_element_type=jnp.float32
    )
    return lax.psum_scatter(mixed.astype(jnp.bfloat16), "head", scatter_dimension=0, tiled=True)


def solution(mesh):
    return jax.shard_map(
        on_device,
        mesh=mesh,
        in_specs=(
            P(("cfg", "seq"), "head"),
            P(("cfg", "seq"), "head"),
            P(("cfg", "seq"), "head"),
            P(("cfg", "seq"), "head"),
            P(("cfg", "seq"), "head"),
            P("cfg"),
            P("cfg"),
            P("cfg", None),
            P("head", None),
        ),
        out_specs=P(("cfg", "seq", "head"), None),
        check_vma=False,
    )
```

```python
import jax
import jax.numpy as jnp
from jax import lax
from jax.experimental import pallas as pl
from jax.experimental.pallas import tpu as pltpu
from jax.sharding import PartitionSpec as P

HD = 128
TILE = 128


NEG = -1e30


def _scores(q_ref, kf0_ref, kf1_ref, ks_ref, j, second, valid):
    sl = slice(j * HD, (j + 1) * HD)
    qj = q_ref[0, :, sl]
    dims = (((1,), (1,)), ((), ()))
    scale = HD ** -0.5
    s0 = lax.dot_general(kf0_ref[0, :, sl], qj, dims, preferred_element_type=jnp.float32) * scale
    s1 = lax.dot_general(kf1_ref[0, :, sl], qj, dims, preferred_element_type=jnp.float32) * scale
    s2 = lax.dot_general(ks_ref[0, :, sl], qj, dims, preferred_element_type=jnp.float32) * scale
    s1 = jnp.where(second > 0, s1, NEG)
    s2 = jnp.where(valid > 0, s2, NEG)
    return s0, s1, s2


def part_kernel(
    fsel_ref, rs_ref, q_ref, kf0_ref, kf1_ref, ks_ref, vf0_ref, vf1_ref, vs_ref, acc_ref, st_ref
):
    heads_part = q_ref.shape[1] // HD
    second = fsel_ref[2]
    valid = rs_ref[1]
    tn = (((0,), (0,)), ((), ()))
    dims = (((1,), (1,)), ((), ()))
    scale = HD ** -0.5
    for j in range(heads_part):
        sl = slice(j * HD, (j + 1) * HD)
        qj = q_ref[:, sl]
        s0 = lax.dot_general(kf0_ref[0, :, sl], qj, dims, preferred_element_type=jnp.float32) * scale
        s1 = lax.dot_general(kf1_ref[0, :, sl], qj, dims, preferred_element_type=jnp.float32) * scale
        s2 = lax.dot_general(ks_ref[0, :, sl], qj, dims, preferred_element_type=jnp.float32) * scale
        s1 = jnp.where(second > 0, s1, NEG)
        s2 = jnp.where(valid > 0, s2, NEG)
        top = jnp.maximum(
            jnp.maximum(jnp.max(s0, axis=0, keepdims=True), jnp.max(s1, axis=0, keepdims=True)),
            jnp.max(s2, axis=0, keepdims=True),
        )
        w0 = jnp.exp(s0 - top)
        w1 = jnp.exp(s1 - top)
        w2 = jnp.exp(s2 - top)
        total = (
            jnp.sum(w0, axis=0, keepdims=True)
            + jnp.sum(w1, axis=0, keepdims=True)
            + jnp.sum(w2, axis=0, keepdims=True)
        )
        summed = (
            lax.dot_general(vf0_ref[0, :, sl], w0.astype(jnp.bfloat16), tn, preferred_element_type=jnp.float32)
            + lax.dot_general(vf1_ref[0, :, sl], w1.astype(jnp.bfloat16), tn, preferred_element_type=jnp.float32)
            + lax.dot_general(vs_ref[0, :, sl], w2.astype(jnp.bfloat16), tn, preferred_element_type=jnp.float32)
        )
        acc_ref[sl, :] = summed.astype(acc_ref.dtype)
        st_ref[0, j : j + 1, :] = top
        st_ref[1, j : j + 1, :] = total


def attend_part(q, fsel, rs, fk3, fv3, sk3, sv3):
    tokens, width = q.shape
    heads_part = width // HD
    full = pl.BlockSpec((tokens, width), lambda i, f, r: (0, 0))
    f0 = pl.BlockSpec((1, TILE, width), lambda i, f, r: (f[0], 0, 0))
    f1 = pl.BlockSpec((1, TILE, width), lambda i, f, r: (f[1], 0, 0))
    st = pl.BlockSpec((1, TILE, width), lambda i, f, r: (r[0], 0, 0))
    return pl.pallas_call(
        part_kernel,
        grid_spec=pltpu.PrefetchScalarGridSpec(
            num_scalar_prefetch=2,
            grid=(1,),
            in_specs=[full, f0, f1, st, f0, f1, st],
            out_specs=[
                pl.BlockSpec((width, tokens), lambda i, f, r: (0, 0)),
                pl.BlockSpec((2, heads_part, tokens), lambda i, f, r: (0, 0, 0)),
            ],
        ),
        out_shape=[
            jax.ShapeDtypeStruct((width, tokens), jnp.bfloat16),
            jax.ShapeDtypeStruct((2, heads_part, tokens), jnp.float32),
        ],
        compiler_params=pltpu.CompilerParams(dimension_semantics=("arbitrary",)),
    )(fsel, rs, q, fk3, fk3, sk3, fv3, fv3, sv3)


def ring_order(n):
    if n == 8:
        return [0, 2, 4, 6, 7, 5, 3, 1]
    return list(range(n))


def combine(run, mine):
    acc_r, stat_r = run
    acc_o, stat_o = mine
    top = jnp.maximum(stat_r[0], stat_o[0])
    f_r = jnp.exp(stat_r[0] - top)
    f_o = jnp.exp(stat_o[0] - top)
    total = stat_r[1] * f_r + stat_o[1] * f_o
    acc = acc_r.astype(jnp.float32) * jnp.repeat(f_r, HD, axis=0) + acc_o.astype(
        jnp.float32
    ) * jnp.repeat(f_o, HD, axis=0)
    return acc, jnp.stack([top, total])


def on_device(
    queries,
    fresh_key,
    fresh_value,
    stale_key,
    stale_value,
    slot_tiles,
    refresh,
    stale_reads,
    out_weight,
):
    tokens_here = queries.shape[0]
    width_here = queries.shape[1]
    heads_here = width_here // HD
    tile_dev = tokens_here // TILE
    readers = stale_reads.shape[0]
    me = lax.axis_index("seq")

    my_refresh = lax.dynamic_slice_in_dim(refresh, me * tile_dev, tile_dev, 0)
    first = jnp.argmax(my_refresh).astype(jnp.int32)
    last = (tile_dev - 1 - jnp.argmax(my_refresh[::-1])).astype(jnp.int32)
    second = (jnp.sum(my_refresh) >= 2).astype(jnp.int32)
    fsel = jnp.stack([first, last, second])

    my_slots = lax.dynamic_slice_in_dim(slot_tiles, me * tile_dev, tile_dev, 0)
    wanted = jnp.take(stale_reads, my_slots, axis=1)
    sidx = jnp.argmax(wanted, axis=1).astype(jnp.int32)
    sval = jnp.max(wanted, axis=1).astype(jnp.int32)

    fk3 = fresh_key.reshape(tile_dev, TILE, width_here)
    fv3 = fresh_value.reshape(tile_dev, TILE, width_here)
    sk3 = stale_key.reshape(tile_dev, TILE, width_here)
    sv3 = stale_value.reshape(tile_dev, TILE, width_here)

    ring = ring_order(readers)
    place = [0] * readers
    for i, d in enumerate(ring):
        place[d] = i
    pos = jnp.array(place, jnp.int32)[me]
    ring_arr = jnp.array(ring, jnp.int32)
    forward = [(ring[i], ring[(i + 1) % readers]) for i in range(readers)]
    backward = [(ring[i], ring[(i - 1) % readers]) for i in range(readers)]
    cut = (heads_here // 2) * HD
    halves = []
    for lo, hi in ((0, cut), (cut, width_here)):
        halves.append(
            (queries[:, lo:hi], fk3[:, :, lo:hi], fv3[:, :, lo:hi], sk3[:, :, lo:hi], sv3[:, :, lo:hi])
        )

    def own(half, q, reader):
        _, k3, v3, s3, t3 = halves[half]
        rs = jnp.stack([sidx[reader], sval[reader]])
        return attend_part(q, fsel, rs, k3, v3, s3, t3)

    moving = [halves[0][0], halves[1][0]]
    run = [None, None]
    perms = (forward, backward)
    for t in range(1, readers):
        got_q = [lax.ppermute(moving[h], "seq", perms[h]) for h in range(2)]
        got_run = [None, None] if t == 1 else [lax.ppermute(run[h], "seq", perms[h]) for h in range(2)]
        readers_t = (ring_arr[(pos - t + readers) % readers], ring_arr[(pos + t) % readers])
        for h in range(2):
            mine = own(h, got_q[h], readers_t[h])
            run[h] = mine if t == 1 else combine(got_run[h], mine)
            run[h] = (run[h][0].astype(jnp.bfloat16), run[h][1])
        moving = got_q
    got_run = [lax.ppermute(run[h], "seq", perms[h]) for h in range(2)]
    run_f = combine(got_run[0], own(0, halves[0][0], me))
    run_b = combine(got_run[1], own(1, halves[1][0], me))
    acc = jnp.concatenate([run_f[0], run_b[0]], axis=0)
    total = jnp.concatenate([run_f[1][1], run_b[1][1]], axis=0)
    attended = (acc / jnp.repeat(total, HD, axis=0)).astype(jnp.bfloat16)
    mixed = lax.dot_general(
        attended, out_weight, (((0,), (0,)), ((), ())), preferred_element_type=jnp.float32
    )
    return lax.psum_scatter(mixed.astype(jnp.bfloat16), "head", scatter_dimension=0, tiled=True)


def solution(mesh):
    return jax.shard_map(
        on_device,
        mesh=mesh,
        in_specs=(
            P(("cfg", "seq"), "head"),
            P(("cfg", "seq"), "head"),
            P(("cfg", "seq"), "head"),
            P(("cfg", "seq"), "head"),
            P(("cfg", "seq"), "head"),
            P("cfg"),
            P("cfg"),
            P("cfg", None),
            P("head", None),
        ),
        out_specs=P(("cfg", "seq", "head"), None),
        check_vma=False,
    )
```

```python
import jax
import jax.numpy as jnp
from jax import lax
from jax.experimental import pallas as pl
from jax.experimental.pallas import tpu as pltpu
from jax.sharding import PartitionSpec as P

HD = 128
TILE = 128


NEG = -1e30


def _scores(q_ref, kf0_ref, kf1_ref, ks_ref, j, second, valid):
    sl = slice(j * HD, (j + 1) * HD)
    qj = q_ref[0, :, sl]
    dims = (((1,), (1,)), ((), ()))
    scale = HD ** -0.5
    s0 = lax.dot_general(kf0_ref[0, :, sl], qj, dims, preferred_element_type=jnp.float32) * scale
    s1 = lax.dot_general(kf1_ref[0, :, sl], qj, dims, preferred_element_type=jnp.float32) * scale
    s2 = lax.dot_general(ks_ref[0, :, sl], qj, dims, preferred_element_type=jnp.float32) * scale
    s1 = jnp.where(second > 0, s1, NEG)
    s2 = jnp.where(valid > 0, s2, NEG)
    return s0, s1, s2


def part_kernel(
    fsel_ref, rs_ref, q_ref, kf0_ref, kf1_ref, ks_ref, vf0_ref, vf1_ref, vs_ref, acc_ref, st_ref
):
    heads_part = q_ref.shape[1] // HD
    second = fsel_ref[2]
    valid = rs_ref[1]
    tn = (((0,), (0,)), ((), ()))
    dims = (((1,), (1,)), ((), ()))
    scale = HD ** -0.5
    def head(j, carry):
        c = pl.multiple_of(j * HD, HD)
        sl = pl.ds(c, HD)
        qj = q_ref[:, sl]
        s0 = lax.dot_general(kf0_ref[0, :, sl], qj, dims, preferred_element_type=jnp.float32) * scale
        s1 = lax.dot_general(kf1_ref[0, :, sl], qj, dims, preferred_element_type=jnp.float32) * scale
        s2 = lax.dot_general(ks_ref[0, :, sl], qj, dims, preferred_element_type=jnp.float32) * scale
        s1 = jnp.where(second > 0, s1, NEG)
        s2 = jnp.where(valid > 0, s2, NEG)
        top = jnp.maximum(
            jnp.maximum(jnp.max(s0, axis=0, keepdims=True), jnp.max(s1, axis=0, keepdims=True)),
            jnp.max(s2, axis=0, keepdims=True),
        )
        w0 = jnp.exp(s0 - top)
        w1 = jnp.exp(s1 - top)
        w2 = jnp.exp(s2 - top)
        total = (
            jnp.sum(w0, axis=0, keepdims=True)
            + jnp.sum(w1, axis=0, keepdims=True)
            + jnp.sum(w2, axis=0, keepdims=True)
        )
        summed = (
            lax.dot_general(vf0_ref[0, :, sl], w0.astype(jnp.bfloat16), tn, preferred_element_type=jnp.float32)
            + lax.dot_general(vf1_ref[0, :, sl], w1.astype(jnp.bfloat16), tn, preferred_element_type=jnp.float32)
            + lax.dot_general(vs_ref[0, :, sl], w2.astype(jnp.bfloat16), tn, preferred_element_type=jnp.float32)
        )
        acc_ref[sl, :] = summed.astype(acc_ref.dtype)
        st_ref[0, pl.ds(j, 1), :] = top
        st_ref[1, pl.ds(j, 1), :] = total
        return carry

    lax.fori_loop(0, heads_part, head, 0)


def attend_part(q, fsel, rs, fk3, fv3, sk3, sv3):
    tokens, width = q.shape
    heads_part = width // HD
    full = pl.BlockSpec((tokens, width), lambda i, f, r: (0, 0))
    f0 = pl.BlockSpec((1, TILE, width), lambda i, f, r: (f[0], 0, 0))
    f1 = pl.BlockSpec((1, TILE, width), lambda i, f, r: (f[1], 0, 0))
    st = pl.BlockSpec((1, TILE, width), lambda i, f, r: (r[0], 0, 0))
    return pl.pallas_call(
        part_kernel,
        grid_spec=pltpu.PrefetchScalarGridSpec(
            num_scalar_prefetch=2,
            grid=(1,),
            in_specs=[full, f0, f1, st, f0, f1, st],
            out_specs=[
                pl.BlockSpec((width, tokens), lambda i, f, r: (0, 0)),
                pl.BlockSpec((2, heads_part, tokens), lambda i, f, r: (0, 0, 0)),
            ],
        ),
        out_shape=[
            jax.ShapeDtypeStruct((width, tokens), jnp.bfloat16),
            jax.ShapeDtypeStruct((2, heads_part, tokens), jnp.float32),
        ],
        compiler_params=pltpu.CompilerParams(dimension_semantics=("arbitrary",)),
    )(fsel, rs, q, fk3, fk3, sk3, fv3, fv3, sv3)


def ring_order(n):
    if n == 8:
        return [0, 2, 4, 6, 7, 5, 3, 1]
    return list(range(n))


def combine(run, mine):
    acc_r, stat_r = run
    acc_o, stat_o = mine
    top = jnp.maximum(stat_r[0], stat_o[0])
    f_r = jnp.exp(stat_r[0] - top)
    f_o = jnp.exp(stat_o[0] - top)
    total = stat_r[1] * f_r + stat_o[1] * f_o
    acc = acc_r.astype(jnp.float32) * jnp.repeat(f_r, HD, axis=0) + acc_o.astype(
        jnp.float32
    ) * jnp.repeat(f_o, HD, axis=0)
    return acc, jnp.stack([top, total])


def on_device(
    queries,
    fresh_key,
    fresh_value,
    stale_key,
    stale_value,
    slot_tiles,
    refresh,
    stale_reads,
    out_weight,
):
    tokens_here = queries.shape[0]
    width_here = queries.shape[1]
    heads_here = width_here // HD
    tile_dev = tokens_here // TILE
    readers = stale_reads.shape[0]
    me = lax.axis_index("seq")

    my_refresh = lax.dynamic_slice_in_dim(refresh, me * tile_dev, tile_dev, 0)
    first = jnp.argmax(my_refresh).astype(jnp.int32)
    last = (tile_dev - 1 - jnp.argmax(my_refresh[::-1])).astype(jnp.int32)
    second = (jnp.sum(my_refresh) >= 2).astype(jnp.int32)
    fsel = jnp.stack([first, last, second])

    my_slots = lax.dynamic_slice_in_dim(slot_tiles, me * tile_dev, tile_dev, 0)
    wanted = jnp.take(stale_reads, my_slots, axis=1)
    sidx = jnp.argmax(wanted, axis=1).astype(jnp.int32)
    sval = jnp.max(wanted, axis=1).astype(jnp.int32)

    fk3 = fresh_key.reshape(tile_dev, TILE, width_here)
    fv3 = fresh_value.reshape(tile_dev, TILE, width_here)
    sk3 = stale_key.reshape(tile_dev, TILE, width_here)
    sv3 = stale_value.reshape(tile_dev, TILE, width_here)

    ring = ring_order(readers)
    place = [0] * readers
    for i, d in enumerate(ring):
        place[d] = i
    pos = jnp.array(place, jnp.int32)[me]
    ring_arr = jnp.array(ring, jnp.int32)
    forward = [(ring[i], ring[(i + 1) % readers]) for i in range(readers)]
    backward = [(ring[i], ring[(i - 1) % readers]) for i in range(readers)]
    cut = (heads_here // 2) * HD
    halves = []
    for lo, hi in ((0, cut), (cut, width_here)):
        halves.append(
            (queries[:, lo:hi], fk3[:, :, lo:hi], fv3[:, :, lo:hi], sk3[:, :, lo:hi], sv3[:, :, lo:hi])
        )

    def own(half, q, reader):
        _, k3, v3, s3, t3 = halves[half]
        rs = jnp.stack([sidx[reader], sval[reader]])
        return attend_part(q, fsel, rs, k3, v3, s3, t3)

    moving = [halves[0][0], halves[1][0]]
    run = [None, None]
    perms = (forward, backward)
    for t in range(1, readers):
        got_q = [lax.ppermute(moving[h], "seq", perms[h]) for h in range(2)]
        got_run = [None, None] if t == 1 else [lax.ppermute(run[h], "seq", perms[h]) for h in range(2)]
        readers_t = (ring_arr[(pos - t + readers) % readers], ring_arr[(pos + t) % readers])
        for h in range(2):
            mine = own(h, got_q[h], readers_t[h])
            run[h] = mine if t == 1 else combine(got_run[h], mine)
            run[h] = (run[h][0].astype(jnp.bfloat16), run[h][1])
        moving = got_q
    got_run = [lax.ppermute(run[h], "seq", perms[h]) for h in range(2)]
    run_f = combine(got_run[0], own(0, halves[0][0], me))
    run_b = combine(got_run[1], own(1, halves[1][0], me))
    acc = jnp.concatenate([run_f[0], run_b[0]], axis=0)
    total = jnp.concatenate([run_f[1][1], run_b[1][1]], axis=0)
    attended = (acc / jnp.repeat(total, HD, axis=0)).astype(jnp.bfloat16)
    mixed = lax.dot_general(
        attended, out_weight, (((0,), (0,)), ((), ())), preferred_element_type=jnp.float32
    )
    return lax.psum_scatter(mixed.astype(jnp.bfloat16), "head", scatter_dimension=0, tiled=True)


def solution(mesh):
    return jax.shard_map(
        on_device,
        mesh=mesh,
        in_specs=(
            P(("cfg", "seq"), "head"),
            P(("cfg", "seq"), "head"),
            P(("cfg", "seq"), "head"),
            P(("cfg", "seq"), "head"),
            P(("cfg", "seq"), "head"),
            P("cfg"),
            P("cfg"),
            P("cfg", None),
            P("head", None),
        ),
        out_specs=P(("cfg", "seq", "head"), None),
        check_vma=False,
    )
```

```python
import jax
import jax.numpy as jnp
from jax import lax
from jax.experimental import pallas as pl
from jax.experimental.pallas import tpu as pltpu
from jax.sharding import PartitionSpec as P

HD = 128
TILE = 128


NEG = -1e30


def _scores(q_ref, kf0_ref, kf1_ref, ks_ref, j, second, valid):
    sl = slice(j * HD, (j + 1) * HD)
    qj = q_ref[0, :, sl]
    dims = (((1,), (1,)), ((), ()))
    scale = HD ** -0.5
    s0 = lax.dot_general(kf0_ref[0, :, sl], qj, dims, preferred_element_type=jnp.float32) * scale
    s1 = lax.dot_general(kf1_ref[0, :, sl], qj, dims, preferred_element_type=jnp.float32) * scale
    s2 = lax.dot_general(ks_ref[0, :, sl], qj, dims, preferred_element_type=jnp.float32) * scale
    s1 = jnp.where(second > 0, s1, NEG)
    s2 = jnp.where(valid > 0, s2, NEG)
    return s0, s1, s2


def part_kernel(
    fsel_ref, rs_ref, q_ref, kf0_ref, kf1_ref, ks_ref, vf0_ref, vf1_ref, vs_ref, acc_ref, st_ref
):
    heads_part = q_ref.shape[1] // HD
    second = fsel_ref[2]
    valid = rs_ref[1]
    tn = (((0,), (0,)), ((), ()))
    dims = (((1,), (1,)), ((), ()))
    scale = HD ** -0.5
    for j in range(heads_part):
        sl = slice(j * HD, (j + 1) * HD)
        qj = q_ref[:, sl]
        s0 = lax.dot_general(kf0_ref[0, :, sl], qj, dims, preferred_element_type=jnp.float32) * scale
        s1 = lax.dot_general(kf1_ref[0, :, sl], qj, dims, preferred_element_type=jnp.float32) * scale
        s2 = lax.dot_general(ks_ref[0, :, sl], qj, dims, preferred_element_type=jnp.float32) * scale
        s1 = jnp.where(second > 0, s1, NEG)
        s2 = jnp.where(valid > 0, s2, NEG)
        top = jnp.maximum(
            jnp.maximum(jnp.max(s0, axis=0, keepdims=True), jnp.max(s1, axis=0, keepdims=True)),
            jnp.max(s2, axis=0, keepdims=True),
        )
        w0 = jnp.exp(s0 - top)
        w1 = jnp.exp(s1 - top)
        w2 = jnp.exp(s2 - top)
        total = (
            jnp.sum(w0, axis=0, keepdims=True)
            + jnp.sum(w1, axis=0, keepdims=True)
            + jnp.sum(w2, axis=0, keepdims=True)
        )
        summed = (
            lax.dot_general(vf0_ref[0, :, sl], w0.astype(jnp.bfloat16), tn, preferred_element_type=jnp.float32)
            + lax.dot_general(vf1_ref[0, :, sl], w1.astype(jnp.bfloat16), tn, preferred_element_type=jnp.float32)
            + lax.dot_general(vs_ref[0, :, sl], w2.astype(jnp.bfloat16), tn, preferred_element_type=jnp.float32)
        )
        acc_ref[sl, :] = summed.astype(acc_ref.dtype)
        st_ref[0, j : j + 1, :] = top
        st_ref[1, j : j + 1, :] = total


def attend_part(q, fsel, rs, fk3, fv3, sk3, sv3):
    tokens, width = q.shape
    heads_part = width // HD
    full = pl.BlockSpec((tokens, width), lambda i, f, r: (0, 0))
    f0 = pl.BlockSpec((1, TILE, width), lambda i, f, r: (f[0], 0, 0))
    f1 = pl.BlockSpec((1, TILE, width), lambda i, f, r: (f[1], 0, 0))
    st = pl.BlockSpec((1, TILE, width), lambda i, f, r: (r[0], 0, 0))
    return pl.pallas_call(
        part_kernel,
        grid_spec=pltpu.PrefetchScalarGridSpec(
            num_scalar_prefetch=2,
            grid=(1,),
            in_specs=[full, f0, f1, st, f0, f1, st],
            out_specs=[
                pl.BlockSpec((width, tokens), lambda i, f, r: (0, 0)),
                pl.BlockSpec((2, heads_part, tokens), lambda i, f, r: (0, 0, 0)),
            ],
        ),
        out_shape=[
            jax.ShapeDtypeStruct((width, tokens), jnp.bfloat16),
            jax.ShapeDtypeStruct((2, heads_part, tokens), jnp.float32),
        ],
        compiler_params=pltpu.CompilerParams(dimension_semantics=("arbitrary",)),
    )(fsel, rs, q, fk3, fk3, sk3, fv3, fv3, sv3)


def ring_order(n):
    if n == 8:
        return [0, 2, 4, 6, 7, 5, 3, 1]
    return list(range(n))


def combine(run, mine):
    acc_r, stat_r = run
    acc_o, stat_o = mine
    top = jnp.maximum(stat_r[0], stat_o[0])
    f_r = jnp.exp(stat_r[0] - top)
    f_o = jnp.exp(stat_o[0] - top)
    total = stat_r[1] * f_r + stat_o[1] * f_o
    acc = acc_r.astype(jnp.float32) * jnp.repeat(f_r, HD, axis=0) + acc_o.astype(
        jnp.float32
    ) * jnp.repeat(f_o, HD, axis=0)
    return acc, jnp.stack([top, total])


def on_device(
    queries,
    fresh_key,
    fresh_value,
    stale_key,
    stale_value,
    slot_tiles,
    refresh,
    stale_reads,
    out_weight,
):
    tokens_here = queries.shape[0]
    width_here = queries.shape[1]
    heads_here = width_here // HD
    tile_dev = tokens_here // TILE
    readers = stale_reads.shape[0]
    me = lax.axis_index("seq")

    my_refresh = lax.dynamic_slice_in_dim(refresh, me * tile_dev, tile_dev, 0)
    first = jnp.argmax(my_refresh).astype(jnp.int32)
    last = (tile_dev - 1 - jnp.argmax(my_refresh[::-1])).astype(jnp.int32)
    second = (jnp.sum(my_refresh) >= 2).astype(jnp.int32)
    fsel = jnp.stack([first, last, second])

    my_slots = lax.dynamic_slice_in_dim(slot_tiles, me * tile_dev, tile_dev, 0)
    wanted = jnp.take(stale_reads, my_slots, axis=1)
    sidx = jnp.argmax(wanted, axis=1).astype(jnp.int32)
    sval = jnp.max(wanted, axis=1).astype(jnp.int32)

    fk3 = fresh_key.reshape(tile_dev, TILE, width_here)
    fv3 = fresh_value.reshape(tile_dev, TILE, width_here)
    sk3 = stale_key.reshape(tile_dev, TILE, width_here)
    sv3 = stale_value.reshape(tile_dev, TILE, width_here)

    ring = ring_order(readers)
    place = [0] * readers
    for i, d in enumerate(ring):
        place[d] = i
    pos = jnp.array(place, jnp.int32)[me]
    ring_arr = jnp.array(ring, jnp.int32)
    forward = [(ring[i], ring[(i + 1) % readers]) for i in range(readers)]
    backward = [(ring[i], ring[(i - 1) % readers]) for i in range(readers)]
    cut = (heads_here // 2) * HD
    halves = []
    for lo, hi in ((0, cut), (cut, width_here)):
        halves.append(
            (queries[:, lo:hi], fk3[:, :, lo:hi], fv3[:, :, lo:hi], sk3[:, :, lo:hi], sv3[:, :, lo:hi])
        )

    def own(half, q, reader):
        _, k3, v3, s3, t3 = halves[half]
        rs = jnp.stack([sidx[reader], sval[reader]])
        return attend_part(q, fsel, rs, k3, v3, s3, t3)

    moving = [halves[0][0], halves[1][0]]
    run = [None, None]
    perms = (forward, backward)
    for t in range(1, readers):
        got_q = [lax.ppermute(moving[h], "seq", perms[h]) for h in range(2)]
        got_run = [None, None] if t == 1 else [lax.ppermute(run[h], "seq", perms[h]) for h in range(2)]
        readers_t = (ring_arr[(pos - t + readers) % readers], ring_arr[(pos + t) % readers])
        for h in range(2):
            mine = own(h, got_q[h], readers_t[h])
            run[h] = mine if t == 1 else combine(got_run[h], mine)
            run[h] = (run[h][0].astype(jnp.bfloat16), run[h][1])
        moving = got_q
    got_run = [lax.ppermute(run[h], "seq", perms[h]) for h in range(2)]
    run_f = combine(got_run[0], own(0, halves[0][0], me))
    run_b = combine(got_run[1], own(1, halves[1][0], me))
    acc = jnp.concatenate([run_f[0], run_b[0]], axis=0)
    total = jnp.concatenate([run_f[1][1], run_b[1][1]], axis=0)
    attended = (acc / jnp.repeat(total, HD, axis=0)).astype(jnp.bfloat16)
    contract = (((0,), (0,)), ((), ()))
    n_head = out_weight.shape[1] // width_here
    if n_head != 2:
        mixed = lax.dot_general(attended, out_weight, contract, preferred_element_type=jnp.float32)
        return lax.psum_scatter(mixed.astype(jnp.bfloat16), "head", scatter_dimension=0, tiled=True)
    rows = tokens_here // 2
    mine_at = lax.axis_index("head") * rows
    theirs = lax.dynamic_slice_in_dim(attended, rows - mine_at, rows, 1)
    ours = lax.dynamic_slice_in_dim(attended, mine_at, rows, 1)
    sent = lax.dot_general(theirs, out_weight, contract, preferred_element_type=jnp.float32)
    got = lax.ppermute(sent.astype(jnp.bfloat16), "head", [(0, 1), (1, 0)])
    kept = lax.dot_general(ours, out_weight, contract, preferred_element_type=jnp.float32)
    return (kept.astype(jnp.bfloat16).astype(jnp.float32) + got.astype(jnp.float32)).astype(jnp.bfloat16)


def solution(mesh):
    return jax.shard_map(
        on_device,
        mesh=mesh,
        in_specs=(
            P(("cfg", "seq"), "head"),
            P(("cfg", "seq"), "head"),
            P(("cfg", "seq"), "head"),
            P(("cfg", "seq"), "head"),
            P(("cfg", "seq"), "head"),
            P("cfg"),
            P("cfg"),
            P("cfg", None),
            P("head", None),
        ),
        out_specs=P(("cfg", "seq", "head"), None),
        check_vma=False,
    )
```

```python
import jax
import jax.numpy as jnp
from jax import lax
from jax.experimental import pallas as pl
from jax.experimental.pallas import tpu as pltpu
from jax.sharding import PartitionSpec as P

HD = 128
TILE = 128


NEG = -1e30


def _scores(q_ref, kf0_ref, kf1_ref, ks_ref, j, second, valid):
    sl = slice(j * HD, (j + 1) * HD)
    qj = q_ref[0, :, sl]
    dims = (((1,), (1,)), ((), ()))
    scale = HD ** -0.5
    s0 = lax.dot_general(kf0_ref[0, :, sl], qj, dims, preferred_element_type=jnp.float32) * scale
    s1 = lax.dot_general(kf1_ref[0, :, sl], qj, dims, preferred_element_type=jnp.float32) * scale
    s2 = lax.dot_general(ks_ref[0, :, sl], qj, dims, preferred_element_type=jnp.float32) * scale
    s1 = jnp.where(second > 0, s1, NEG)
    s2 = jnp.where(valid > 0, s2, NEG)
    return s0, s1, s2


def part_kernel(
    fsel_ref, rs_ref, q_ref, kf0_ref, kf1_ref, ks_ref, vf0_ref, vf1_ref, vs_ref, acc_ref, st_ref
):
    heads_part = q_ref.shape[1] // HD
    second = fsel_ref[2]
    valid = rs_ref[1]
    tn = (((0,), (0,)), ((), ()))
    dims = (((1,), (1,)), ((), ()))
    scale = HD ** -0.5
    for j in range(heads_part):
        sl = slice(j * HD, (j + 1) * HD)
        qj = q_ref[:, sl]
        s0 = lax.dot_general(kf0_ref[0, :, sl], qj, dims, preferred_element_type=jnp.float32) * scale
        s1 = lax.dot_general(kf1_ref[0, :, sl], qj, dims, preferred_element_type=jnp.float32) * scale
        s2 = lax.dot_general(ks_ref[0, :, sl], qj, dims, preferred_element_type=jnp.float32) * scale
        s1 = jnp.where(second > 0, s1, NEG)
        s2 = jnp.where(valid > 0, s2, NEG)
        top = jnp.maximum(
            jnp.maximum(jnp.max(s0, axis=0, keepdims=True), jnp.max(s1, axis=0, keepdims=True)),
            jnp.max(s2, axis=0, keepdims=True),
        )
        w0 = jnp.exp(s0 - top)
        w1 = jnp.exp(s1 - top)
        w2 = jnp.exp(s2 - top)
        total = (
            jnp.sum(w0, axis=0, keepdims=True)
            + jnp.sum(w1, axis=0, keepdims=True)
            + jnp.sum(w2, axis=0, keepdims=True)
        )
        summed = (
            lax.dot_general(vf0_ref[0, :, sl], w0.astype(jnp.bfloat16), tn, preferred_element_type=jnp.float32)
            + lax.dot_general(vf1_ref[0, :, sl], w1.astype(jnp.bfloat16), tn, preferred_element_type=jnp.float32)
            + lax.dot_general(vs_ref[0, :, sl], w2.astype(jnp.bfloat16), tn, preferred_element_type=jnp.float32)
        )
        acc_ref[sl, :] = summed.astype(acc_ref.dtype)
        st_ref[0, j : j + 1, :] = top
        st_ref[1, j : j + 1, :] = total


def attend_part(q, fsel, rs, fk3, fv3, sk3, sv3):
    tokens, width = q.shape
    heads_part = width // HD
    full = pl.BlockSpec((tokens, width), lambda i, f, r: (0, 0))
    f0 = pl.BlockSpec((1, TILE, width), lambda i, f, r: (f[0], 0, 0))
    f1 = pl.BlockSpec((1, TILE, width), lambda i, f, r: (f[1], 0, 0))
    st = pl.BlockSpec((1, TILE, width), lambda i, f, r: (r[0], 0, 0))
    return pl.pallas_call(
        part_kernel,
        grid_spec=pltpu.PrefetchScalarGridSpec(
            num_scalar_prefetch=2,
            grid=(1,),
            in_specs=[full, f0, f1, st, f0, f1, st],
            out_specs=[
                pl.BlockSpec((width, tokens), lambda i, f, r: (0, 0)),
                pl.BlockSpec((2, heads_part, tokens), lambda i, f, r: (0, 0, 0)),
            ],
        ),
        out_shape=[
            jax.ShapeDtypeStruct((width, tokens), jnp.bfloat16),
            jax.ShapeDtypeStruct((2, heads_part, tokens), jnp.float32),
        ],
        compiler_params=pltpu.CompilerParams(dimension_semantics=("arbitrary",)),
    )(fsel, rs, q, fk3, fk3, sk3, fv3, fv3, sv3)


def ring_order(n):
    if n == 8:
        return [0, 2, 4, 6, 7, 5, 3, 1]
    return list(range(n))


def combine(run, mine):
    acc_r, stat_r = run
    acc_o, stat_o = mine
    top = jnp.maximum(stat_r[0], stat_o[0])
    f_r = jnp.exp(stat_r[0] - top)
    f_o = jnp.exp(stat_o[0] - top)
    total = stat_r[1] * f_r + stat_o[1] * f_o
    acc = acc_r.astype(jnp.float32) * jnp.repeat(f_r, HD, axis=0) + acc_o.astype(
        jnp.float32
    ) * jnp.repeat(f_o, HD, axis=0)
    return acc, jnp.stack([top, total])


def on_device(
    queries,
    fresh_key,
    fresh_value,
    stale_key,
    stale_value,
    slot_tiles,
    refresh,
    stale_reads,
    out_weight,
):
    tokens_here = queries.shape[0]
    width_here = queries.shape[1]
    heads_here = width_here // HD
    tile_dev = tokens_here // TILE
    readers = stale_reads.shape[0]
    me = lax.axis_index("seq")

    my_refresh = lax.dynamic_slice_in_dim(refresh, me * tile_dev, tile_dev, 0)
    first = jnp.argmax(my_refresh).astype(jnp.int32)
    last = (tile_dev - 1 - jnp.argmax(my_refresh[::-1])).astype(jnp.int32)
    second = (jnp.sum(my_refresh) >= 2).astype(jnp.int32)
    fsel = jnp.stack([first, last, second])

    my_slots = lax.dynamic_slice_in_dim(slot_tiles, me * tile_dev, tile_dev, 0)
    wanted = jnp.take(stale_reads, my_slots, axis=1)
    sidx = jnp.argmax(wanted, axis=1).astype(jnp.int32)
    sval = jnp.max(wanted, axis=1).astype(jnp.int32)

    fk3 = fresh_key.reshape(tile_dev, TILE, width_here)
    fv3 = fresh_value.reshape(tile_dev, TILE, width_here)
    sk3 = stale_key.reshape(tile_dev, TILE, width_here)
    sv3 = stale_value.reshape(tile_dev, TILE, width_here)

    ring = ring_order(readers)
    place = [0] * readers
    for i, d in enumerate(ring):
        place[d] = i
    pos = jnp.array(place, jnp.int32)[me]
    ring_arr = jnp.array(ring, jnp.int32)
    forward = [(ring[i], ring[(i + 1) % readers]) for i in range(readers)]
    backward = [(ring[i], ring[(i - 1) % readers]) for i in range(readers)]
    cut = (heads_here // 2) * HD
    halves = []
    for lo, hi in ((0, cut), (cut, width_here)):
        halves.append(
            (queries[:, lo:hi], fk3[:, :, lo:hi], fv3[:, :, lo:hi], sk3[:, :, lo:hi], sv3[:, :, lo:hi])
        )

    def own(half, q, reader):
        _, k3, v3, s3, t3 = halves[half]
        rs = jnp.stack([sidx[reader], sval[reader]])
        return attend_part(q, fsel, rs, k3, v3, s3, t3)

    moving = [halves[0][0], halves[1][0]]
    run = [None, None]
    perms = (forward, backward)
    for t in range(1, readers):
        got_q = [lax.ppermute(moving[h], "seq", perms[h]) for h in range(2)]
        got_run = [None, None] if t == 1 else [lax.ppermute(run[h], "seq", perms[h]) for h in range(2)]
        readers_t = (ring_arr[(pos - t + readers) % readers], ring_arr[(pos + t) % readers])
        for h in range(2):
            mine = own(h, got_q[h], readers_t[h])
            run[h] = mine if t == 1 else combine(got_run[h], mine)
            run[h] = (run[h][0].astype(jnp.bfloat16), run[h][1])
        moving = got_q
    got_run = [lax.ppermute(run[h], "seq", perms[h]) for h in range(2)]
    run_f = combine(got_run[0], own(0, halves[0][0], me))
    run_b = combine(got_run[1], own(1, halves[1][0], me))
    acc = jnp.concatenate([run_f[0], run_b[0]], axis=0)
    total = jnp.concatenate([run_f[1][1], run_b[1][1]], axis=0)
    attended = (acc / jnp.repeat(total, HD, axis=0)).astype(jnp.bfloat16)
    contract = (((0,), (0,)), ((), ()))
    n_head = out_weight.shape[1] // width_here
    if n_head != 2:
        mixed = lax.dot_general(attended, out_weight, contract, preferred_element_type=jnp.float32)
        return lax.psum_scatter(mixed.astype(jnp.bfloat16), "head", scatter_dimension=0, tiled=True)
    rows = tokens_here // 2
    mine_at = lax.axis_index("head") * rows
    theirs = lax.dynamic_slice_in_dim(attended, rows - mine_at, rows, 1)
    ours = lax.dynamic_slice_in_dim(attended, mine_at, rows, 1)
    half = out_weight.shape[1] // 2
    got = []
    for lo in (0, half):
        sent = lax.dot_general(
            theirs, out_weight[:, lo : lo + half], contract, preferred_element_type=jnp.float32
        )
        got.append(lax.ppermute(sent.astype(jnp.bfloat16), "head", [(0, 1), (1, 0)]))
    got = jnp.concatenate(got, axis=1)
    kept = lax.dot_general(ours, out_weight, contract, preferred_element_type=jnp.float32)
    kept = lax.optimization_barrier(kept.astype(jnp.bfloat16))
    return (kept.astype(jnp.float32) + got.astype(jnp.float32)).astype(jnp.bfloat16)


def solution(mesh):
    return jax.shard_map(
        on_device,
        mesh=mesh,
        in_specs=(
            P(("cfg", "seq"), "head"),
            P(("cfg", "seq"), "head"),
            P(("cfg", "seq"), "head"),
            P(("cfg", "seq"), "head"),
            P(("cfg", "seq"), "head"),
            P("cfg"),
            P("cfg"),
            P("cfg", None),
            P("head", None),
        ),
        out_specs=P(("cfg", "seq", "head"), None),
        check_vma=False,
    )
```

```python
import jax
import jax.numpy as jnp
from jax import lax
from jax.experimental import pallas as pl
from jax.experimental.pallas import tpu as pltpu
from jax.sharding import PartitionSpec as P

HD = 128
TILE = 128


NEG = -1e30


def _scores(q_ref, kf0_ref, kf1_ref, ks_ref, j, second, valid):
    sl = slice(j * HD, (j + 1) * HD)
    qj = q_ref[0, :, sl]
    dims = (((1,), (1,)), ((), ()))
    scale = HD ** -0.5
    s0 = lax.dot_general(kf0_ref[0, :, sl], qj, dims, preferred_element_type=jnp.float32) * scale
    s1 = lax.dot_general(kf1_ref[0, :, sl], qj, dims, preferred_element_type=jnp.float32) * scale
    s2 = lax.dot_general(ks_ref[0, :, sl], qj, dims, preferred_element_type=jnp.float32) * scale
    s1 = jnp.where(second > 0, s1, NEG)
    s2 = jnp.where(valid > 0, s2, NEG)
    return s0, s1, s2


def part_kernel(
    fsel_ref, rs_ref, q_ref, kf0_ref, kf1_ref, ks_ref, vf0_ref, vf1_ref, vs_ref, acc_ref, st_ref
):
    heads_part = q_ref.shape[1] // HD
    second = fsel_ref[2]
    valid = rs_ref[1]
    tn = (((0,), (0,)), ((), ()))
    dims = (((1,), (1,)), ((), ()))
    scale = HD ** -0.5
    def head(j, carry):
        c = pl.multiple_of(j * HD, HD)
        sl = pl.ds(c, HD)
        qj = q_ref[:, sl]
        s0 = lax.dot_general(kf0_ref[0, :, sl], qj, dims, preferred_element_type=jnp.float32) * scale
        s1 = lax.dot_general(kf1_ref[0, :, sl], qj, dims, preferred_element_type=jnp.float32) * scale
        s2 = lax.dot_general(ks_ref[0, :, sl], qj, dims, preferred_element_type=jnp.float32) * scale
        s1 = jnp.where(second > 0, s1, NEG)
        s2 = jnp.where(valid > 0, s2, NEG)
        top = jnp.maximum(
            jnp.maximum(jnp.max(s0, axis=0, keepdims=True), jnp.max(s1, axis=0, keepdims=True)),
            jnp.max(s2, axis=0, keepdims=True),
        )
        w0 = jnp.exp(s0 - top)
        w1 = jnp.exp(s1 - top)
        w2 = jnp.exp(s2 - top)
        total = (
            jnp.sum(w0, axis=0, keepdims=True)
            + jnp.sum(w1, axis=0, keepdims=True)
            + jnp.sum(w2, axis=0, keepdims=True)
        )
        summed = (
            lax.dot_general(vf0_ref[0, :, sl], w0.astype(jnp.bfloat16), tn, preferred_element_type=jnp.float32)
            + lax.dot_general(vf1_ref[0, :, sl], w1.astype(jnp.bfloat16), tn, preferred_element_type=jnp.float32)
            + lax.dot_general(vs_ref[0, :, sl], w2.astype(jnp.bfloat16), tn, preferred_element_type=jnp.float32)
        )
        acc_ref[sl, :] = summed.astype(acc_ref.dtype)
        st_ref[0, pl.ds(j, 1), :] = top
        st_ref[1, pl.ds(j, 1), :] = total
        return carry

    lax.fori_loop(0, heads_part, head, 0)


def attend_part(q, fsel, rs, fk3, fv3, sk3, sv3):
    tokens, width = q.shape
    heads_part = width // HD
    full = pl.BlockSpec((tokens, width), lambda i, f, r: (0, 0))
    f0 = pl.BlockSpec((1, TILE, width), lambda i, f, r: (f[0], 0, 0))
    f1 = pl.BlockSpec((1, TILE, width), lambda i, f, r: (f[1], 0, 0))
    st = pl.BlockSpec((1, TILE, width), lambda i, f, r: (r[0], 0, 0))
    return pl.pallas_call(
        part_kernel,
        grid_spec=pltpu.PrefetchScalarGridSpec(
            num_scalar_prefetch=2,
            grid=(1,),
            in_specs=[full, f0, f1, st, f0, f1, st],
            out_specs=[
                pl.BlockSpec((width, tokens), lambda i, f, r: (0, 0)),
                pl.BlockSpec((2, heads_part, tokens), lambda i, f, r: (0, 0, 0)),
            ],
        ),
        out_shape=[
            jax.ShapeDtypeStruct((width, tokens), jnp.bfloat16),
            jax.ShapeDtypeStruct((2, heads_part, tokens), jnp.float32),
        ],
        compiler_params=pltpu.CompilerParams(dimension_semantics=("arbitrary",)),
    )(fsel, rs, q, fk3, fk3, sk3, fv3, fv3, sv3)


def ring_order(n):
    if n == 8:
        return [0, 2, 4, 6, 7, 5, 3, 1]
    return list(range(n))


def combine(run, mine):
    acc_r, stat_r = run
    acc_o, stat_o = mine
    top = jnp.maximum(stat_r[0], stat_o[0])
    f_r = jnp.exp(stat_r[0] - top)
    f_o = jnp.exp(stat_o[0] - top)
    total = stat_r[1] * f_r + stat_o[1] * f_o
    acc = acc_r.astype(jnp.float32) * jnp.repeat(f_r, HD, axis=0) + acc_o.astype(
        jnp.float32
    ) * jnp.repeat(f_o, HD, axis=0)
    return acc, jnp.stack([top, total])


def on_device(
    queries,
    fresh_key,
    fresh_value,
    stale_key,
    stale_value,
    slot_tiles,
    refresh,
    stale_reads,
    out_weight,
):
    tokens_here = queries.shape[0]
    width_here = queries.shape[1]
    heads_here = width_here // HD
    tile_dev = tokens_here // TILE
    readers = stale_reads.shape[0]
    me = lax.axis_index("seq")

    my_refresh = lax.dynamic_slice_in_dim(refresh, me * tile_dev, tile_dev, 0)
    first = jnp.argmax(my_refresh).astype(jnp.int32)
    last = (tile_dev - 1 - jnp.argmax(my_refresh[::-1])).astype(jnp.int32)
    second = (jnp.sum(my_refresh) >= 2).astype(jnp.int32)
    fsel = jnp.stack([first, last, second])

    my_slots = lax.dynamic_slice_in_dim(slot_tiles, me * tile_dev, tile_dev, 0)
    wanted = jnp.take(stale_reads, my_slots, axis=1)
    sidx = jnp.argmax(wanted, axis=1).astype(jnp.int32)
    sval = jnp.max(wanted, axis=1).astype(jnp.int32)

    fk3 = fresh_key.reshape(tile_dev, TILE, width_here)
    fv3 = fresh_value.reshape(tile_dev, TILE, width_here)
    sk3 = stale_key.reshape(tile_dev, TILE, width_here)
    sv3 = stale_value.reshape(tile_dev, TILE, width_here)

    ring = ring_order(readers)
    place = [0] * readers
    for i, d in enumerate(ring):
        place[d] = i
    pos = jnp.array(place, jnp.int32)[me]
    ring_arr = jnp.array(ring, jnp.int32)
    forward = [(ring[i], ring[(i + 1) % readers]) for i in range(readers)]
    backward = [(ring[i], ring[(i - 1) % readers]) for i in range(readers)]
    cut = (heads_here // 2) * HD
    halves = []
    for lo, hi in ((0, cut), (cut, width_here)):
        halves.append(
            (queries[:, lo:hi], fk3[:, :, lo:hi], fv3[:, :, lo:hi], sk3[:, :, lo:hi], sv3[:, :, lo:hi])
        )

    def own(half, q, reader):
        _, k3, v3, s3, t3 = halves[half]
        rs = jnp.stack([sidx[reader], sval[reader]])
        return attend_part(q, fsel, rs, k3, v3, s3, t3)

    perms = (forward, backward)

    def run_ring(q_part):
        mine = [q_part[:, :cut], q_part[:, cut:]]
        moving = list(mine)
        run = [None, None]
        for t in range(1, readers):
            got_q = [lax.ppermute(moving[h], "seq", perms[h]) for h in range(2)]
            got_run = [None, None] if t == 1 else [lax.ppermute(run[h], "seq", perms[h]) for h in range(2)]
            readers_t = (ring_arr[(pos - t + readers) % readers], ring_arr[(pos + t) % readers])
            for h in range(2):
                part = own(h, got_q[h], readers_t[h])
                run[h] = part if t == 1 else combine(got_run[h], part)
                run[h] = (run[h][0].astype(jnp.bfloat16), run[h][1])
            moving = got_q
        got_run = [lax.ppermute(run[h], "seq", perms[h]) for h in range(2)]
        fin = [combine(got_run[h], own(h, mine[h], me)) for h in range(2)]
        acc = jnp.concatenate([fin[0][0], fin[1][0]], axis=0)
        total = jnp.concatenate([fin[0][1][1], fin[1][1][1]], axis=0)
        return (acc / jnp.repeat(total, HD, axis=0)).astype(jnp.bfloat16)

    contract = (((0,), (0,)), ((), ()))
    n_head = out_weight.shape[1] // width_here
    rows = tokens_here // 2
    big = tokens_here - TILE
    if n_head != 2 or big < rows:
        attended = run_ring(queries)
        mixed = lax.dot_general(attended, out_weight, contract, preferred_element_type=jnp.float32)
        return lax.psum_scatter(mixed.astype(jnp.bfloat16), "head", scatter_dimension=0, tiled=True)
    hid = lax.axis_index("head")
    start1 = (1 - hid) * TILE
    start2 = hid * big
    first = run_ring(lax.dynamic_slice_in_dim(queries, start1, big, 0))
    theirs = lax.dynamic_slice_in_dim(first, (1 - hid) * (big - rows), rows, 1)
    sent = lax.dot_general(theirs, out_weight, contract, preferred_element_type=jnp.float32)
    got = lax.ppermute(sent.astype(jnp.bfloat16), "head", [(0, 1), (1, 0)])
    first, rest_q = lax.optimization_barrier(
        (first, lax.dynamic_slice_in_dim(queries, start2, TILE, 0))
    )
    second = run_ring(rest_q)
    full = jnp.zeros((width_here, tokens_here), jnp.bfloat16)
    full = lax.dynamic_update_slice_in_dim(full, first, start1, 1)
    full = lax.dynamic_update_slice_in_dim(full, second, start2, 1)
    ours = lax.dynamic_slice_in_dim(full, hid * rows, rows, 1)
    kept = lax.dot_general(ours, out_weight, contract, preferred_element_type=jnp.float32)
    return (kept.astype(jnp.bfloat16).astype(jnp.float32) + got.astype(jnp.float32)).astype(jnp.bfloat16)


def solution(mesh):
    return jax.shard_map(
        on_device,
        mesh=mesh,
        in_specs=(
            P(("cfg", "seq"), "head"),
            P(("cfg", "seq"), "head"),
            P(("cfg", "seq"), "head"),
            P(("cfg", "seq"), "head"),
            P(("cfg", "seq"), "head"),
            P("cfg"),
            P("cfg"),
            P("cfg", None),
            P("head", None),
        ),
        out_specs=P(("cfg", "seq", "head"), None),
        check_vma=False,
    )
```

```python
import jax
import jax.numpy as jnp
from jax import lax
from jax.experimental import pallas as pl
from jax.experimental.pallas import tpu as pltpu
from jax.sharding import PartitionSpec as P

HD = 128
TILE = 128


NEG = -1e30


def _scores(q_ref, kf0_ref, kf1_ref, ks_ref, j, second, valid):
    sl = slice(j * HD, (j + 1) * HD)
    qj = q_ref[0, :, sl]
    dims = (((1,), (1,)), ((), ()))
    scale = HD ** -0.5
    s0 = lax.dot_general(kf0_ref[0, :, sl], qj, dims, preferred_element_type=jnp.float32) * scale
    s1 = lax.dot_general(kf1_ref[0, :, sl], qj, dims, preferred_element_type=jnp.float32) * scale
    s2 = lax.dot_general(ks_ref[0, :, sl], qj, dims, preferred_element_type=jnp.float32) * scale
    s1 = jnp.where(second > 0, s1, NEG)
    s2 = jnp.where(valid > 0, s2, NEG)
    return s0, s1, s2


def part_kernel(
    fsel_ref, rs_ref, q_ref, kf0_ref, kf1_ref, ks_ref, vf0_ref, vf1_ref, vs_ref, acc_ref, st_ref
):
    heads_part = q_ref.shape[1] // HD
    second = fsel_ref[2]
    valid = rs_ref[1]
    tn = (((0,), (0,)), ((), ()))
    dims = (((1,), (1,)), ((), ()))
    scale = HD ** -0.5
    for j in range(heads_part):
        sl = slice(j * HD, (j + 1) * HD)
        qj = q_ref[:, sl]
        s0 = lax.dot_general(kf0_ref[0, :, sl], qj, dims, preferred_element_type=jnp.float32) * scale
        s1 = lax.dot_general(kf1_ref[0, :, sl], qj, dims, preferred_element_type=jnp.float32) * scale
        s2 = lax.dot_general(ks_ref[0, :, sl], qj, dims, preferred_element_type=jnp.float32) * scale
        s1 = jnp.where(second > 0, s1, NEG)
        s2 = jnp.where(valid > 0, s2, NEG)
        top = jnp.maximum(
            jnp.maximum(jnp.max(s0, axis=0, keepdims=True), jnp.max(s1, axis=0, keepdims=True)),
            jnp.max(s2, axis=0, keepdims=True),
        )
        w0 = jnp.exp(s0 - top)
        w1 = jnp.exp(s1 - top)
        w2 = jnp.exp(s2 - top)
        total = (
            jnp.sum(w0, axis=0, keepdims=True)
            + jnp.sum(w1, axis=0, keepdims=True)
            + jnp.sum(w2, axis=0, keepdims=True)
        )
        summed = (
            lax.dot_general(vf0_ref[0, :, sl], w0.astype(jnp.bfloat16), tn, preferred_element_type=jnp.float32)
            + lax.dot_general(vf1_ref[0, :, sl], w1.astype(jnp.bfloat16), tn, preferred_element_type=jnp.float32)
            + lax.dot_general(vs_ref[0, :, sl], w2.astype(jnp.bfloat16), tn, preferred_element_type=jnp.float32)
        )
        acc_ref[sl, :] = summed.astype(acc_ref.dtype)
        st_ref[0, j : j + 1, :] = top
        st_ref[1, j : j + 1, :] = total


def attend_part(q, fsel, rs, fk3, fv3, sk3, sv3):
    tokens, width = q.shape
    heads_part = width // HD
    full = pl.BlockSpec((tokens, width), lambda i, f, r: (0, 0))
    f0 = pl.BlockSpec((1, TILE, width), lambda i, f, r: (f[0], 0, 0))
    f1 = pl.BlockSpec((1, TILE, width), lambda i, f, r: (f[1], 0, 0))
    st = pl.BlockSpec((1, TILE, width), lambda i, f, r: (r[0], 0, 0))
    return pl.pallas_call(
        part_kernel,
        grid_spec=pltpu.PrefetchScalarGridSpec(
            num_scalar_prefetch=2,
            grid=(1,),
            in_specs=[full, f0, f1, st, f0, f1, st],
            out_specs=[
                pl.BlockSpec((width, tokens), lambda i, f, r: (0, 0)),
                pl.BlockSpec((2, heads_part, tokens), lambda i, f, r: (0, 0, 0)),
            ],
        ),
        out_shape=[
            jax.ShapeDtypeStruct((width, tokens), jnp.bfloat16),
            jax.ShapeDtypeStruct((2, heads_part, tokens), jnp.float32),
        ],
        compiler_params=pltpu.CompilerParams(dimension_semantics=("arbitrary",)),
    )(fsel, rs, q, fk3, fk3, sk3, fv3, fv3, sv3)


def ring_order(n):
    if n == 8:
        return [0, 2, 4, 6, 7, 5, 3, 1]
    return list(range(n))


def combine(run, mine):
    acc_r, stat_r = run
    acc_o, stat_o = mine
    top = jnp.maximum(stat_r[0], stat_o[0])
    f_r = jnp.exp(stat_r[0] - top)
    f_o = jnp.exp(stat_o[0] - top)
    total = stat_r[1] * f_r + stat_o[1] * f_o
    acc = acc_r.astype(jnp.float32) * jnp.repeat(f_r, HD, axis=0) + acc_o.astype(
        jnp.float32
    ) * jnp.repeat(f_o, HD, axis=0)
    return acc, jnp.stack([top, total])


def on_device(
    queries,
    fresh_key,
    fresh_value,
    stale_key,
    stale_value,
    slot_tiles,
    refresh,
    stale_reads,
    out_weight,
):
    tokens_here = queries.shape[0]
    width_here = queries.shape[1]
    heads_here = width_here // HD
    tile_dev = tokens_here // TILE
    readers = stale_reads.shape[0]
    me = lax.axis_index("seq")

    my_refresh = lax.dynamic_slice_in_dim(refresh, me * tile_dev, tile_dev, 0)
    first = jnp.argmax(my_refresh).astype(jnp.int32)
    last = (tile_dev - 1 - jnp.argmax(my_refresh[::-1])).astype(jnp.int32)
    second = (jnp.sum(my_refresh) >= 2).astype(jnp.int32)
    fsel = jnp.stack([first, last, second])

    my_slots = lax.dynamic_slice_in_dim(slot_tiles, me * tile_dev, tile_dev, 0)
    wanted = jnp.take(stale_reads, my_slots, axis=1)
    sidx = jnp.argmax(wanted, axis=1).astype(jnp.int32)
    sval = jnp.max(wanted, axis=1).astype(jnp.int32)

    fk3 = fresh_key.reshape(tile_dev, TILE, width_here)
    fv3 = fresh_value.reshape(tile_dev, TILE, width_here)
    sk3 = stale_key.reshape(tile_dev, TILE, width_here)
    sv3 = stale_value.reshape(tile_dev, TILE, width_here)

    ring = ring_order(readers)
    place = [0] * readers
    for i, d in enumerate(ring):
        place[d] = i
    pos = jnp.array(place, jnp.int32)[me]
    ring_arr = jnp.array(ring, jnp.int32)
    forward = [(ring[i], ring[(i + 1) % readers]) for i in range(readers)]
    backward = [(ring[i], ring[(i - 1) % readers]) for i in range(readers)]
    cut = (heads_here // 2) * HD
    halves = []
    for lo, hi in ((0, cut), (cut, width_here)):
        halves.append(
            (queries[:, lo:hi], fk3[:, :, lo:hi], fv3[:, :, lo:hi], sk3[:, :, lo:hi], sv3[:, :, lo:hi])
        )

    steps = jnp.arange(readers + 1, dtype=jnp.int32)
    met = jnp.stack(
        [ring_arr[(pos - steps + 2 * readers) % readers], ring_arr[(pos + steps) % readers]]
    )
    table = jnp.stack([sidx[met], sval[met]], axis=-1)

    def own(half, q, step):
        _, k3, v3, s3, t3 = halves[half]
        return attend_part(q, fsel, table[half, step], k3, v3, s3, t3)

    moving = [halves[0][0], halves[1][0]]
    run = [None, None]
    perms = (forward, backward)
    for t in range(1, readers):
        got_q = [lax.ppermute(moving[h], "seq", perms[h]) for h in range(2)]
        got_run = [None, None] if t == 1 else [lax.ppermute(run[h], "seq", perms[h]) for h in range(2)]
        for h in range(2):
            mine = own(h, got_q[h], t)
            run[h] = mine if t == 1 else combine(got_run[h], mine)
            run[h] = (run[h][0].astype(jnp.bfloat16), run[h][1])
        moving = got_q
    got_run = [lax.ppermute(run[h], "seq", perms[h]) for h in range(2)]
    run_f = combine(got_run[0], own(0, halves[0][0], readers))
    run_b = combine(got_run[1], own(1, halves[1][0], readers))
    acc = jnp.concatenate([run_f[0], run_b[0]], axis=0)
    total = jnp.concatenate([run_f[1][1], run_b[1][1]], axis=0)
    attended = (acc / jnp.repeat(total, HD, axis=0)).astype(jnp.bfloat16)
    contract = (((0,), (0,)), ((), ()))
    n_head = out_weight.shape[1] // width_here
    if n_head != 2:
        mixed = lax.dot_general(attended, out_weight, contract, preferred_element_type=jnp.float32)
        return lax.psum_scatter(mixed.astype(jnp.bfloat16), "head", scatter_dimension=0, tiled=True)
    rows = tokens_here // 2
    mine_at = lax.axis_index("head") * rows
    theirs = lax.dynamic_slice_in_dim(attended, rows - mine_at, rows, 1)
    ours = lax.dynamic_slice_in_dim(attended, mine_at, rows, 1)
    half = out_weight.shape[1] // 2
    got = []
    for lo in (0, half):
        sent = lax.dot_general(
            theirs, out_weight[:, lo : lo + half], contract, preferred_element_type=jnp.float32
        )
        got.append(lax.ppermute(sent.astype(jnp.bfloat16), "head", [(0, 1), (1, 0)]))
    got = jnp.concatenate(got, axis=1)
    kept = lax.dot_general(ours, out_weight, contract, preferred_element_type=jnp.float32)
    kept = lax.optimization_barrier(kept.astype(jnp.bfloat16))
    return (kept.astype(jnp.float32) + got.astype(jnp.float32)).astype(jnp.bfloat16)


def solution(mesh):
    return jax.shard_map(
        on_device,
        mesh=mesh,
        in_specs=(
            P(("cfg", "seq"), "head"),
            P(("cfg", "seq"), "head"),
            P(("cfg", "seq"), "head"),
            P(("cfg", "seq"), "head"),
            P(("cfg", "seq"), "head"),
            P("cfg"),
            P("cfg"),
            P("cfg", None),
            P("head", None),
        ),
        out_specs=P(("cfg", "seq", "head"), None),
        check_vma=False,
    )
```

```python
import jax
import jax.numpy as jnp
from jax import lax
from jax.experimental import pallas as pl
from jax.experimental.pallas import tpu as pltpu
from jax.sharding import PartitionSpec as P

HD = 128
TILE = 128


NEG = -1e30


def _scores(q_ref, kf0_ref, kf1_ref, ks_ref, j, second, valid):
    sl = slice(j * HD, (j + 1) * HD)
    qj = q_ref[0, :, sl]
    dims = (((1,), (1,)), ((), ()))
    scale = HD ** -0.5
    s0 = lax.dot_general(kf0_ref[0, :, sl], qj, dims, preferred_element_type=jnp.float32) * scale
    s1 = lax.dot_general(kf1_ref[0, :, sl], qj, dims, preferred_element_type=jnp.float32) * scale
    s2 = lax.dot_general(ks_ref[0, :, sl], qj, dims, preferred_element_type=jnp.float32) * scale
    s1 = jnp.where(second > 0, s1, NEG)
    s2 = jnp.where(valid > 0, s2, NEG)
    return s0, s1, s2


def part_kernel(
    fsel_ref, rs_ref, q_ref, kf0_ref, kf1_ref, ks_ref, vf0_ref, vf1_ref, vs_ref, acc_ref, st_ref
):
    heads_part = q_ref.shape[1] // HD
    second = fsel_ref[2]
    valid = rs_ref[1]
    tn = (((0,), (0,)), ((), ()))
    dims = (((1,), (1,)), ((), ()))
    scale = HD ** -0.5
    for j in range(heads_part):
        sl = slice(j * HD, (j + 1) * HD)
        qj = q_ref[:, sl]
        s0 = lax.dot_general(kf0_ref[0, :, sl], qj, dims, preferred_element_type=jnp.float32) * scale
        s1 = lax.dot_general(kf1_ref[0, :, sl], qj, dims, preferred_element_type=jnp.float32) * scale
        s2 = lax.dot_general(ks_ref[0, :, sl], qj, dims, preferred_element_type=jnp.float32) * scale
        s1 = jnp.where(second > 0, s1, NEG)
        s2 = jnp.where(valid > 0, s2, NEG)
        top = jnp.maximum(
            jnp.maximum(jnp.max(s0, axis=0, keepdims=True), jnp.max(s1, axis=0, keepdims=True)),
            jnp.max(s2, axis=0, keepdims=True),
        )
        w0 = jnp.exp(s0 - top)
        w1 = jnp.exp(s1 - top)
        w2 = jnp.exp(s2 - top)
        total = (
            jnp.sum(w0, axis=0, keepdims=True)
            + jnp.sum(w1, axis=0, keepdims=True)
            + jnp.sum(w2, axis=0, keepdims=True)
        )
        summed = (
            lax.dot_general(vf0_ref[0, :, sl], w0.astype(jnp.bfloat16), tn, preferred_element_type=jnp.float32)
            + lax.dot_general(vf1_ref[0, :, sl], w1.astype(jnp.bfloat16), tn, preferred_element_type=jnp.float32)
            + lax.dot_general(vs_ref[0, :, sl], w2.astype(jnp.bfloat16), tn, preferred_element_type=jnp.float32)
        )
        acc_ref[sl, :] = summed.astype(acc_ref.dtype)
        st_ref[0, j : j + 1, :] = top
        st_ref[1, j : j + 1, :] = total


def attend_part(q, fsel, rs, fk3, fv3, sk3, sv3):
    tokens, width = q.shape
    heads_part = width // HD
    full = pl.BlockSpec((tokens, width), lambda i, f, r: (0, 0))
    f0 = pl.BlockSpec((1, TILE, width), lambda i, f, r: (f[0], 0, 0))
    f1 = pl.BlockSpec((1, TILE, width), lambda i, f, r: (f[1], 0, 0))
    st = pl.BlockSpec((1, TILE, width), lambda i, f, r: (r[0], 0, 0))
    return pl.pallas_call(
        part_kernel,
        grid_spec=pltpu.PrefetchScalarGridSpec(
            num_scalar_prefetch=2,
            grid=(1,),
            in_specs=[full, f0, f1, st, f0, f1, st],
            out_specs=[
                pl.BlockSpec((width, tokens), lambda i, f, r: (0, 0)),
                pl.BlockSpec((2, heads_part, tokens), lambda i, f, r: (0, 0, 0)),
            ],
        ),
        out_shape=[
            jax.ShapeDtypeStruct((width, tokens), jnp.bfloat16),
            jax.ShapeDtypeStruct((2, heads_part, tokens), jnp.float32),
        ],
        compiler_params=pltpu.CompilerParams(dimension_semantics=("arbitrary",)),
    )(fsel, rs, q, fk3, fk3, sk3, fv3, fv3, sv3)


def ring_order(n):
    if n == 8:
        return [0, 2, 4, 6, 7, 5, 3, 1]
    return list(range(n))


def combine(run, mine):
    acc_r, stat_r = run
    acc_o, stat_o = mine
    top = jnp.maximum(stat_r[0], stat_o[0])
    f_r = jnp.exp(stat_r[0] - top)
    f_o = jnp.exp(stat_o[0] - top)
    total = stat_r[1] * f_r + stat_o[1] * f_o
    acc = acc_r.astype(jnp.float32) * jnp.repeat(f_r, HD, axis=0) + acc_o.astype(
        jnp.float32
    ) * jnp.repeat(f_o, HD, axis=0)
    return acc, jnp.stack([top, total])


def on_device(
    queries,
    fresh_key,
    fresh_value,
    stale_key,
    stale_value,
    slot_tiles,
    refresh,
    stale_reads,
    out_weight,
):
    tokens_here = queries.shape[0]
    width_here = queries.shape[1]
    heads_here = width_here // HD
    tile_dev = tokens_here // TILE
    readers = stale_reads.shape[0]
    me = lax.axis_index("seq")

    my_refresh = lax.dynamic_slice_in_dim(refresh, me * tile_dev, tile_dev, 0)
    first = jnp.argmax(my_refresh).astype(jnp.int32)
    last = (tile_dev - 1 - jnp.argmax(my_refresh[::-1])).astype(jnp.int32)
    second = (jnp.sum(my_refresh) >= 2).astype(jnp.int32)
    fsel = jnp.stack([first, last, second])

    my_slots = lax.dynamic_slice_in_dim(slot_tiles, me * tile_dev, tile_dev, 0)
    wanted = jnp.take(stale_reads, my_slots, axis=1)
    sidx = jnp.argmax(wanted, axis=1).astype(jnp.int32)
    sval = jnp.max(wanted, axis=1).astype(jnp.int32)

    fk3 = fresh_key.reshape(tile_dev, TILE, width_here)
    fv3 = fresh_value.reshape(tile_dev, TILE, width_here)
    sk3 = stale_key.reshape(tile_dev, TILE, width_here)
    sv3 = stale_value.reshape(tile_dev, TILE, width_here)

    ring = ring_order(readers)
    place = [0] * readers
    for i, d in enumerate(ring):
        place[d] = i
    pos = jnp.array(place, jnp.int32)[me]
    ring_arr = jnp.array(ring, jnp.int32)
    forward = [(ring[i], ring[(i + 1) % readers]) for i in range(readers)]
    backward = [(ring[i], ring[(i - 1) % readers]) for i in range(readers)]
    cut = (heads_here // 2) * HD
    halves = []
    for lo, hi in ((0, cut), (cut, width_here)):
        halves.append(
            (queries[:, lo:hi], fk3[:, :, lo:hi], fv3[:, :, lo:hi], sk3[:, :, lo:hi], sv3[:, :, lo:hi])
        )

    steps = jnp.arange(readers + 1, dtype=jnp.int32)
    met = jnp.stack(
        [ring_arr[(pos - steps + 2 * readers) % readers], ring_arr[(pos + steps) % readers]]
    )
    table = jnp.stack([sidx[met], sval[met]], axis=-1)

    def own(half, q, step):
        _, k3, v3, s3, t3 = halves[half]
        return attend_part(q, fsel, table[half, step], k3, v3, s3, t3)

    moving = [halves[0][0], halves[1][0]]
    run = [None, None]
    perms = (forward, backward)
    for t in range(1, readers):
        got_q = [lax.ppermute(moving[h], "seq", perms[h]) for h in range(2)]
        got_run = [None, None] if t == 1 else [lax.ppermute(run[h], "seq", perms[h]) for h in range(2)]
        for h in range(2):
            mine = own(h, got_q[h], t)
            run[h] = mine if t == 1 else combine(got_run[h], mine)
            run[h] = (run[h][0].astype(jnp.bfloat16), run[h][1])
        moving = got_q
    got_run = [lax.ppermute(run[h], "seq", perms[h]) for h in range(2)]
    run_f = combine(got_run[0], own(0, halves[0][0], readers))
    run_b = combine(got_run[1], own(1, halves[1][0], readers))
    acc = jnp.concatenate([run_f[0], run_b[0]], axis=0)
    total = jnp.concatenate([run_f[1][1], run_b[1][1]], axis=0)
    attended = (acc / jnp.repeat(total, HD, axis=0)).astype(jnp.bfloat16)
    contract = (((0,), (0,)), ((), ()))
    n_head = out_weight.shape[1] // width_here
    if n_head != 2:
        mixed = lax.dot_general(attended, out_weight, contract, preferred_element_type=jnp.float32)
        return lax.psum_scatter(mixed.astype(jnp.bfloat16), "head", scatter_dimension=0, tiled=True)
    rows = tokens_here // 2
    mine_at = lax.axis_index("head") * rows
    theirs = lax.dynamic_slice_in_dim(attended, rows - mine_at, rows, 1)
    ours = lax.dynamic_slice_in_dim(attended, mine_at, rows, 1)
    sent = lax.dot_general(theirs, out_weight, contract, preferred_element_type=jnp.float32)
    got = lax.ppermute(sent.astype(jnp.bfloat16), "head", [(0, 1), (1, 0)])
    kept = lax.dot_general(ours, out_weight, contract, preferred_element_type=jnp.float32)
    kept = lax.optimization_barrier(kept.astype(jnp.bfloat16))
    return (kept.astype(jnp.float32) + got.astype(jnp.float32)).astype(jnp.bfloat16)


def solution(mesh):
    return jax.shard_map(
        on_device,
        mesh=mesh,
        in_specs=(
            P(("cfg", "seq"), "head"),
            P(("cfg", "seq"), "head"),
            P(("cfg", "seq"), "head"),
            P(("cfg", "seq"), "head"),
            P(("cfg", "seq"), "head"),
            P("cfg"),
            P("cfg"),
            P("cfg", None),
            P("head", None),
        ),
        out_specs=P(("cfg", "seq", "head"), None),
        check_vma=False,
    )
```
